32 devices in a mesh: dp: 4 (over y, x), expert: 2 (over core), tensor: 4 (over z).
Axes of the slice: x: 2, y: 2, z: 4, core: 2. Of those that a mesh axis runs over, the one named last changes fastest.
Arguments:
- tokens: bfloat16 [4096, 2048], P(('dp', 'expert', 'tensor')), may hold values from -6 to 6
- norm_gain: float32 [2048], replicated, may hold values from 0.1 to 1.9
- expert_ids: int32 [4096, 8], P(('dp', 'expert', 'tensor')), may hold values from 0 to 31, all different within a row; in each aligned block of 128 rows (0 to 127, 128 to 255, ...) at most 64 rows name the same one
- gate_weights: float32 [4096, 8], P(('dp', 'expert', 'tensor')), may hold values from 0.03 to 0.4
- w_in: bfloat16 [32, 2048, 1536], P(('dp', 'expert', 'tensor')), may hold values from -1.875 to 1.875, as said below
- scale_in: float32 [32, 16, 12], P(('dp', 'expert', 'tensor')), may hold values from 0.03 to 0.12
- w_out: bfloat16 [32, 768, 2048], P(('dp', 'expert', 'tensor')), may hold values from -1.875 to 1.875, as said below
- scale_out: float32 [32, 6, 16], P(('dp', 'expert', 'tensor')), may hold values from 0.02 to 0.08
- w_sync: bfloat16 [2048, 2, 2048], P(None, None, 'tensor'), may hold values from -0.125 to 0.125
- head_weight: float32 [16], P('tensor'), may hold values from -3 to 3
- frame_rows: int32 [8, 2, 256], P(('dp', 'expert')), may hold values from 0 to 511, as said below
- lag_offsets: int32 [21], replicated, may hold values from -32 to 32, as said below
Outputs:
- mixed: bfloat16 [4096, 2048], P(('dp', 'expert', 'tensor'))
- sync_logits: float32 [8, 21], P(('dp', 'expert'))
The draws below stay inside these ranges and needn't reach their ends.
Inputs may be any that keep to these rules, and one draw needn't show every extreme that they name: `expert_ids`: in each aligned block of 128 rows (the rows of one device) no expert is named by more than 64 of the block's choices; the choices of a row are different. `w_in`: every entry is an e4m3 value: a sign times (1 + m / 8) times 2 to the e, with whole m of 0 to 7 and e of -3 to 0. `w_out`: every entry is an e4m3 value: a sign times (1 + m / 8) times 2 to the e, with whole m of 0 to 7 and e of -3 to 0. `frame_rows`: for each clip the audio rows and the video rows together are each of 0 to 511 once. `lag_offsets`: 21 different lags in increasing order; the first is -32 and the last 32.
All inputs are finite; a program needn't handle non-finite values.
Results may differ from the reference program's by a relative error of at most 0.0035.
The reference program's roundings to bfloat16 on the way count: a program that leaves them out, or rounds other values in their place, can miss the bound.
Values may be sent and summed in bfloat16 or wider, within the bound.
No kernel may reach another device: no remote copies, remote signals or barrier semaphores. Data moves between devices by JAX's collectives and lax.ppermute only.
A program may use at most 128 MiB of HBM per device.

```python
import math
import jax
import jax.numpy as jnp
import numpy as np
from jax import lax

D = 2048
FF = 768
TOP = 8
QB = 128
HEADS = 16
HD = 128
LAGS = 21
LAGMAX = 32
TOK_DEV = 128
EXPERTS = 32
TOKENS = 4096
MOST = 64
CLIP = 512
CLIPS = 8
FRAMES = 256
DEVICES = 32


def e4m3_values(key, shape):
    key_mant, key_expo, key_sign = jax.random.split(key, 3)
    mantissa = jax.random.randint(key_mant, shape, 0, 8).astype(jnp.float32)
    exponent = jax.random.randint(key_expo, shape, -3, 1).astype(jnp.float32)
    sign = (jax.random.randint(key_sign, shape, 0, 2) * 2 - 1).astype(jnp.float32)
    return (sign * (1.0 + mantissa / 8.0) * jnp.exp2(exponent)).astype(jnp.float32)


def draw_w_in(key, part):
    return e4m3_values(jax.random.fold_in(key, 31), (EXPERTS, D, 2 * FF)).astype(jnp.bfloat16)


def draw_w_out(key, part):
    return e4m3_values(jax.random.fold_in(key, 37), (EXPERTS, FF, D)).astype(jnp.bfloat16)


def draw_frame_rows(key, part):
    keys = jax.random.split(jax.random.fold_in(key, 11), CLIPS)
    orders = jax.vmap(lambda one: jax.random.permutation(one, CLIP))(keys)
    return orders.reshape(CLIPS, 2, FRAMES).astype(jnp.int32)


def draw_lag_offsets(key, part):
    inner = jax.random.permutation(jax.random.fold_in(key, 23), 2 * LAGMAX - 1) - (LAGMAX - 1)
    chosen = inner[:LAGS - 2]
    ends = jnp.array([-LAGMAX, LAGMAX], dtype=jnp.int32)
    return jnp.sort(jnp.concatenate([ends, chosen.astype(jnp.int32)])).astype(jnp.int32)


def level_of(stream_key, extent, cuts, smallest, top_value):
    factor_of, own = 1.0, jax.random.fold_in(stream_key, 6)
    for dim, shards_of in cuts:
        draws = jnp.exp(jax.random.uniform(jax.random.fold_in(own, dim), (shards_of,), jnp.float32, smallest / len(cuts), top_value / len(cuts)))
        factor_of = factor_of * jnp.repeat(draws, extent[dim] // shards_of).reshape([-1 if axis == dim else 1 for axis in range(len(extent))])
    return factor_of


def deal_out(own_key, own, number, rows, count, top, bound, skew):
    sequence = jax.random.permutation(own_key, count)
    packed, common = portions_of(count, rows * top, bound, skew, True), portions_of(count, rows * top, bound, skew, False)
    places = jnp.arange(count)

    def named(lengths, turn):
        used = int((lengths > 0).sum())
        fixed = max(1, used // 4)
        passed = fixed + (places - fixed + turn * (used - fixed)) % max(1, count - fixed)
        return jnp.zeros((count,), jnp.int32).at[sequence[jnp.where(places < fixed, places, passed)]].set(jnp.asarray(lengths, jnp.int32))

    lengths = jnp.where(number % 4 == 0, named(packed, number // 4), named(common, number - number // 4 - 1))
    mixed = jax.random.permutation(jax.random.fold_in(own, 3), count)
    donor, taker = mixed[0:count // 2 * 2:2], mixed[1:count // 2 * 2:2]
    margin = jnp.minimum(lengths[donor] - 1, bound - lengths[taker]) // 2
    margin = jnp.where((donor == sequence[0]) | (taker == sequence[0]) | (lengths[taker] == 0), 0, jnp.maximum(margin, 0))
    passed = jax.random.randint(jax.random.fold_in(own, 4), (count // 2,), 0, 1 << 20) % (margin + 1)
    lengths = lengths.at[donor].add(-passed).at[taker].add(passed)
    members = jnp.searchsorted(jnp.cumsum(lengths), jnp.arange(rows * top), side="right").astype(jnp.int32)
    grid = members.reshape(top, rows).T
    grid = grid[jax.random.permutation(jax.random.fold_in(own, 1), rows)]
    turn = jax.random.randint(jax.random.fold_in(own, 2), (rows, 1), 0, top)
    return jnp.take_along_axis(grid, (jnp.arange(top)[None, :] + turn) % top, axis=1)


def portions_of(number_of, total, most, skew, full):
    portions = [(1 << 20) // math.isqrt(standing ** skew) + 1 for standing in range(1, number_of + 1)]
    largest = most if full else min(most, max(-(-total // number_of), total * portions[0] // sum(portions)))
    least = 1 if total - largest >= number_of - 1 else 0
    given, surplus = [largest] + [least] * (number_of - 1), total - largest - least * (number_of - 1)
    while surplus > 0:
        movable = [i for i in range(1, number_of) if given[i] < largest] or [i for i in range(1, number_of) if given[i] < most]
        pool, remaining = sum([portions[i] for i in movable]), surplus
        for i in movable:
            extra = min(most - given[i], max(1, remaining * portions[i] // pool), surplus)
            given[i] = given[i] + extra
            surplus = surplus - extra
    return np.array(given)


def scatter_about(own_key, extent, deviation, limit, cuts=(), held_as=jnp.bfloat16):
    drawn = deviation * jax.random.normal(own_key, extent, jnp.float32)
    if cuts:
        drawn = drawn * level_of(own_key, extent, cuts, -0.22, 0.18)
    return jnp.clip(drawn, -limit, limit).astype(held_as)


def setup_inputs(seed: int = 0) -> dict:
    key_of = jax.random.split(jax.random.key(seed), 13)
    tokens = scatter_about(key_of[0], (TOKENS, D), 1.0, 6.0, ((0, 32),))
    norm_gain = jnp.clip(1.0 + 0.18 * jax.random.normal(key_of[1], (D,), jnp.float32), 0.1, 1.9)
    expert_ids_keys = jax.random.split(jax.random.fold_in(key_of[2], 1), TOKENS // TOK_DEV)
    expert_ids_turns = jax.random.permutation(jax.random.fold_in(key_of[2], 3), TOKENS // TOK_DEV)
    expert_ids = jax.vmap(lambda own, number: deal_out(jax.random.fold_in(key_of[2], 2), own, number, TOK_DEV, EXPERTS, TOP, MOST, 2))(expert_ids_keys, expert_ids_turns).reshape((TOKENS, TOP))
    gate_weights = jnp.clip(jnp.exp(math.log(0.4) - 2.5902672 * jax.random.uniform(key_of[3], (TOKENS, TOP), jnp.float32) ** level_of(key_of[3], (TOKENS, TOP), ((0, 32),), -0.2, 0.2)), 0.03, 0.4)
    w_in = draw_w_in(jax.random.fold_in(key_of[12], 71), 0)
    scale_in = jnp.clip(jnp.exp(math.log(0.12) - 1.3862944 * jax.random.uniform(key_of[5], (EXPERTS, D // QB, 2 * FF // QB), jnp.float32) ** level_of(key_of[5], (EXPERTS, D // QB, 2 * FF // QB), ((0, 32),), -0.2, 0.2)), 0.03, 0.12)
    w_out = draw_w_out(jax.random.fold_in(key_of[12], 71), 0)
    scale_out = jnp.clip(jnp.exp(math.log(0.08) - 1.3862944 * jax.random.uniform(key_of[7], (EXPERTS, FF // QB, D // QB), jnp.float32) ** level_of(key_of[7], (EXPERTS, FF // QB, D // QB), ((0, 32),), -0.2, 0.2)), 0.02, 0.08)
    w_sync = scatter_about(key_of[8], (D, 2, HEADS * HD), D ** -0.5, 0.125, ((2, 4),))
    head_weight = scatter_about(key_of[9], (HEADS,), 0.5, 3.0, ((0, 4),), jnp.float32)
    frame_rows = draw_frame_rows(jax.random.fold_in(key_of[12], 71), 0)
    lag_offsets = draw_lag_offsets(jax.random.fold_in(key_of[12], 71), 0)
    return dict(tokens=tokens, norm_gain=norm_gain, expert_ids=expert_ids, gate_weights=gate_weights, w_in=w_in, scale_in=scale_in, w_out=w_out, scale_out=scale_out, w_sync=w_sync, head_weight=head_weight, frame_rows=frame_rows, lag_offsets=lag_offsets)


def dequant(weights, scales):
    full = jnp.repeat(jnp.repeat(scales, QB, axis=0), QB, axis=1)
    return (weights.astype(jnp.float32) * full).astype(jnp.bfloat16)

def reference(tokens, norm_gain, expert_ids, gate_weights, w_in, scale_in, w_out, scale_out, w_sync, head_weight, frame_rows, lag_offsets):
    x_float = tokens.astype(jnp.float32)
    normed = (x_float * lax.rsqrt(lax.optimization_barrier(jnp.mean(x_float * x_float, axis=-1, keepdims=True)) + 1e-06) * norm_gain).astype(jnp.bfloat16)
    flat_ids = expert_ids.reshape(-1)
    flat_gate = gate_weights.reshape(-1)
    capacity = DEVICES * MOST
    pairs = TOKENS * TOP

    def one_expert(total, which):
        found = jnp.nonzero(flat_ids == which, size=capacity, fill_value=pairs)[0].astype(jnp.int32)
        token_rows = jnp.minimum(found // TOP, TOKENS - 1).astype(jnp.int32)
        inputs = normed[token_rows]
        gate_up = jnp.dot(inputs, dequant(w_in[which], scale_in[which]), preferred_element_type=jnp.float32)
        hidden = (jax.nn.silu(gate_up[:, :FF]) * gate_up[:, FF:]).astype(jnp.bfloat16)
        output = jnp.dot(hidden, dequant(w_out[which], scale_out[which]), preferred_element_type=jnp.float32).astype(jnp.bfloat16)
        weight = jnp.where(found < pairs, flat_gate[jnp.minimum(found, pairs - 1)], jnp.zeros((), jnp.float32))
        total = total.at[token_rows].add(weight[:, None] * output.astype(jnp.float32))
        return (total, None)
    combined, _ = lax.scan(one_expert, jnp.zeros((TOKENS, D), jnp.float32), jnp.arange(EXPERTS, dtype=jnp.int32))
    mixed = (x_float + combined).astype(jnp.bfloat16)
    proj = jnp.dot(mixed, w_sync.reshape(D, 2 * HEADS * HD), preferred_element_type=jnp.float32).astype(jnp.bfloat16)
    clips = proj.reshape(CLIPS, CLIP, 2 * HEADS * HD)
    times = jnp.arange(FRAMES, dtype=jnp.int32)
    shifted = times[None, :] + lag_offsets[:, None]
    valid = (shifted >= 0) & (shifted < FRAMES)
    clamped = jnp.clip(shifted, 0, FRAMES - 1).astype(jnp.int32)
    time_grid = jnp.broadcast_to(times[None, :], clamped.shape)
    counts = (FRAMES - jnp.abs(lag_offsets)).astype(jnp.float32)

    def clip_score(item):
        clip_rows, rows_of = item
        audio = clip_rows[rows_of[0], :HEADS * HD].reshape(FRAMES, HEADS, HD).astype(jnp.float32)
        video = clip_rows[rows_of[1], HEADS * HD:].reshape(FRAMES, HEADS, HD).astype(jnp.float32)
        grams = jnp.einsum('thd,shd->hts', audio, video)
        picked = grams[:, time_grid, clamped]
        sums = lax.optimization_barrier(jnp.sum(jnp.where(valid[None], picked, 0.0), axis=-1))
        score = sums / jnp.sqrt(counts * HD)[None, :]
        return lax.optimization_barrier(jnp.sum(head_weight[:, None] * score, axis=0))
    sync_logits = lax.map(clip_score, (clips, frame_rows))
    return (mixed, sync_logits)
```

```python
import jax
import jax.numpy as jnp
from jax import lax
from jax.sharding import PartitionSpec as P


def dequant(weights, scales):
    block = weights.shape[0] // scales.shape[0]
    full = jnp.repeat(jnp.repeat(scales, block, axis=0), block, axis=1)
    return (weights.astype(jnp.float32) * full).astype(jnp.bfloat16)


def shards(
    tokens,
    norm_gain,
    expert_ids,
    gate_weights,
    w_in,
    scale_in,
    w_out,
    scale_out,
    w_sync,
    head_weight,
    frame_rows,
    lag_offsets,
):
    rows, width = tokens.shape
    top = expert_ids.shape[1]
    lines = lax.axis_size("tensor")
    plane = lax.axis_size(("dp", "expert"))
    experts_all = plane * lines * w_in.shape[0]
    most = 2 * rows * top // experts_all
    cap = lines * most
    here = lax.axis_index("tensor")
    x_float = tokens.astype(jnp.float32)
    normed = (
        x_float * lax.rsqrt(jnp.mean(x_float * x_float, axis=-1, keepdims=True) + 1e-06) * norm_gain
    ).astype(jnp.bfloat16)

    flat_ids = expert_ids.reshape(-1)
    pair_count = rows * top
    onehot = (flat_ids[:, None] == jnp.arange(experts_all, dtype=jnp.int32)[None, :]).astype(
        jnp.bfloat16
    )
    pair_index = jnp.arange(pair_count, dtype=jnp.int32)
    earlier = (pair_index[None, :] < pair_index[:, None]).astype(jnp.bfloat16)
    before = jnp.dot(earlier, onehot, preferred_element_type=jnp.float32)
    slots = jnp.sum(before * onehot.astype(jnp.float32), axis=1).reshape(rows, top)
    routing = jnp.concatenate(
        [expert_ids.astype(jnp.float32), slots, gate_weights.astype(jnp.float32)], axis=1
    )

    line_normed = lax.all_gather(normed, "tensor", axis=0, tiled=True)
    line_routing = lax.all_gather(routing, "tensor", axis=0, tiled=False)
    ids_l = line_routing[:, :, :top].astype(jnp.int32)
    slot_l = line_routing[:, :, top : 2 * top].astype(jnp.int32)
    gate_l = line_routing[:, :, 2 * top :]
    mine = (ids_l % lines) == here
    target = jnp.where(mine, (ids_l // lines) * most + slot_l, -1)
    slot_ids = jnp.arange(plane * most, dtype=jnp.int32)
    match = target[:, None, :, :] == slot_ids[None, :, None, None]
    select = jnp.any(match, axis=3)
    weight = jnp.sum(jnp.where(match, gate_l[:, None, :, :], 0.0), axis=3)
    same = (
        jnp.arange(lines, dtype=jnp.int32)[:, None] == jnp.arange(lines, dtype=jnp.int32)[None, :]
    )
    select = select.reshape(lines, plane, most, rows)
    select_full = (
        select.transpose(1, 0, 2, 3)[:, :, :, None, :] & same[None, :, None, :, None]
    ).reshape(plane * cap, lines * rows)
    weight = weight.reshape(lines, plane, most, rows).transpose(1, 0, 2, 3)
    weight_full = jnp.where(
        same[None, :, None, :, None], weight[:, :, :, None, :], 0.0
    ).reshape(plane * cap, lines * rows)
    outgoing = jnp.dot(
        select_full.astype(jnp.bfloat16), line_normed, preferred_element_type=jnp.float32
    ).astype(jnp.bfloat16)
    outgoing = outgoing.reshape(plane, cap, width)

    gate_up = dequant(w_in[0], scale_in[0])
    down_proj = dequant(w_out[0], scale_out[0])
    hidden_width = down_proj.shape[0]
    block = lax.all_to_all(outgoing, ("dp", "expert"), split_axis=0, concat_axis=0, tiled=True)
    flat = block.reshape(-1, width)
    mixed_in = jnp.dot(flat, gate_up, preferred_element_type=jnp.float32)
    hidden = (jax.nn.silu(mixed_in[:, :hidden_width]) * mixed_in[:, hidden_width:]).astype(
        jnp.bfloat16
    )
    output = jnp.dot(hidden, down_proj, preferred_element_type=jnp.float32).astype(jnp.bfloat16)
    send_block = output.reshape(block.shape)
    back = lax.all_to_all(send_block, ("dp", "expert"), split_axis=0, concat_axis=0, tiled=True)
    back = back.reshape(-1, width)

    weight_top = lax.reduce_precision(weight_full, exponent_bits=8, mantissa_bits=7)
    weight_hi = weight_top.astype(jnp.bfloat16)
    weight_lo = (weight_full - weight_top).astype(jnp.bfloat16)
    contract = (((0,), (0,)), ((), ()))
    partial = lax.dot_general(
        weight_hi, back, contract, preferred_element_type=jnp.float32
    ) + lax.dot_general(weight_lo, back, contract, preferred_element_type=jnp.float32)
    combined = lax.psum_scatter(partial, "tensor", scatter_dimension=0, tiled=True)
    mixed = (x_float + combined).astype(jnp.bfloat16)

    local_sync = w_sync.reshape(width, -1)
    proj = jnp.dot(
        lax.all_gather(mixed, "tensor", axis=0, tiled=True),
        local_sync,
        preferred_element_type=jnp.float32,
    ).astype(jnp.bfloat16)
    half = proj.shape[1] // 2
    heads_here = head_weight.shape[0]
    head_size = half // heads_here
    frames = frame_rows.shape[2]
    clip_len = proj.shape[0]
    clip_index = jnp.arange(clip_len, dtype=jnp.int32)
    pick_audio = (frame_rows[0, 0][:, None] == clip_index[None, :]).astype(jnp.bfloat16)
    pick_video = (frame_rows[0, 1][:, None] == clip_index[None, :]).astype(jnp.bfloat16)
    audio = (
        jnp.dot(pick_audio, proj[:, :half], preferred_element_type=jnp.float32)
        .astype(jnp.bfloat16)
        .reshape(frames, heads_here, head_size)
    )
    video = (
        jnp.dot(pick_video, proj[:, half:], preferred_element_type=jnp.float32)
        .astype(jnp.bfloat16)
        .reshape(frames, heads_here, head_size)
    )
    grams = jnp.einsum("thd,shd->hts", audio, video, preferred_element_type=jnp.float32)
    times = jnp.arange(frames, dtype=jnp.int32)
    offsets = times[None, :] - times[:, None]
    diagonal = (
        (offsets[None, :, :] == lag_offsets[:, None, None])
        .astype(jnp.float32)
        .reshape(lag_offsets.shape[0], frames * frames)
    )
    sums = lax.dot_general(
        grams.reshape(heads_here, frames * frames),
        diagonal,
        (((1,), (1,)), ((), ())),
        precision=lax.Precision.HIGHEST,
        preferred_element_type=jnp.float32,
    )
    counts = (frames - jnp.abs(lag_offsets)).astype(jnp.float32)
    score = sums / jnp.sqrt(counts * head_size)[None, :]
    partial_logits = jnp.sum(head_weight[:, None] * score, axis=0)
    sync_logits = lax.psum(partial_logits, "tensor")
    return (mixed, sync_logits[None, :])


def solution(mesh):
    return jax.shard_map(
        shards,
        mesh=mesh,
        in_specs=(
            P(("dp", "expert", "tensor"), None),
            P(),
            P(("dp", "expert", "tensor"), None),
            P(("dp", "expert", "tensor"), None),
            P(("dp", "expert", "tensor"), None, None),
            P(("dp", "expert", "tensor"), None, None),
            P(("dp", "expert", "tensor"), None, None),
            P(("dp", "expert", "tensor"), None, None),
            P(None, None, "tensor"),
            P("tensor"),
            P(("dp", "expert"), None, None),
            P(),
        ),
        out_specs=(P(("dp", "expert", "tensor"), None), P(("dp", "expert"), None)),
        check_vma=False,
    )
```

```python
import jax
import jax.numpy as jnp
from jax import lax
from jax.sharding import PartitionSpec as P


def dequant(weights, scales):
    block = weights.shape[0] // scales.shape[0]
    full = jnp.repeat(jnp.repeat(scales, block, axis=0), block, axis=1)
    return (weights.astype(jnp.float32) * full).astype(jnp.bfloat16)


def shards(
    tokens,
    norm_gain,
    expert_ids,
    gate_weights,
    w_in,
    scale_in,
    w_out,
    scale_out,
    w_sync,
    head_weight,
    frame_rows,
    lag_offsets,
):
    rows, width = tokens.shape
    top = expert_ids.shape[1]
    lines = lax.axis_size("tensor")
    plane = lax.axis_size(("dp", "expert"))
    experts_all = plane * lines * w_in.shape[0]
    most = 2 * rows * top // experts_all
    cap = lines * most
    here = lax.axis_index("tensor")
    x_float = tokens.astype(jnp.float32)
    normed = (
        x_float * lax.rsqrt(jnp.mean(x_float * x_float, axis=-1, keepdims=True) + 1e-06) * norm_gain
    ).astype(jnp.bfloat16)

    flat_ids = expert_ids.reshape(-1)
    pair_count = rows * top
    onehot = (flat_ids[:, None] == jnp.arange(experts_all, dtype=jnp.int32)[None, :]).astype(
        jnp.bfloat16
    )
    pair_index = jnp.arange(pair_count, dtype=jnp.int32)
    earlier = (pair_index[None, :] < pair_index[:, None]).astype(jnp.bfloat16)
    before = jnp.dot(earlier, onehot, preferred_element_type=jnp.float32)
    slots = jnp.sum(before * onehot.astype(jnp.float32), axis=1).reshape(rows, top)
    gate = gate_weights.astype(jnp.float32)
    gate_top = lax.reduce_precision(gate, exponent_bits=8, mantissa_bits=7)
    routing = jnp.concatenate(
        [
            expert_ids.astype(jnp.bfloat16),
            slots.astype(jnp.bfloat16),
            gate_top.astype(jnp.bfloat16),
            (gate - gate_top).astype(jnp.bfloat16),
        ],
        axis=1,
    )
    extra = rows * 4 * top // width
    padded = rows + 16
    packed = jnp.concatenate(
        [
            normed,
            routing.reshape(extra, width),
            jnp.zeros((padded - rows - extra, width), jnp.bfloat16),
        ],
        axis=0,
    )
    line = lax.all_gather(packed, "tensor", axis=0, tiled=False)
    line_routing = line[:, rows : rows + extra, :].reshape(lines, rows, 4 * top)
    ids_l = line_routing[:, :, :top].astype(jnp.int32)
    slot_l = line_routing[:, :, top : 2 * top].astype(jnp.int32)
    gate_hi = line_routing[:, :, 2 * top : 3 * top].astype(jnp.float32)
    gate_lo = line_routing[:, :, 3 * top :].astype(jnp.float32)
    mine = (ids_l % lines) == here
    target = jnp.where(mine, (ids_l // lines) * most + slot_l, -1)
    slot_ids = jnp.arange(plane * most, dtype=jnp.int32)
    match = target[:, None, :, :] == slot_ids[None, :, None, None]
    select = jnp.any(match, axis=3)
    weight_hi = jnp.sum(jnp.where(match, gate_hi[:, None, :, :], 0.0), axis=3)
    weight_lo = jnp.sum(jnp.where(match, gate_lo[:, None, :, :], 0.0), axis=3)
    same = (
        jnp.arange(lines, dtype=jnp.int32)[:, None] == jnp.arange(lines, dtype=jnp.int32)[None, :]
    )
    select = select.reshape(lines, plane, most, rows).transpose(1, 0, 2, 3)
    select = jnp.pad(select, ((0, 0), (0, 0), (0, 0), (0, padded - rows)))
    select_full = (
        (select[:, :, :, None, :] & same[None, :, None, :, None])
        .reshape(plane * cap, lines * padded)
        .astype(jnp.bfloat16)
    )

    def spread(weight):
        weight = weight.reshape(lines, plane, most, rows).transpose(1, 0, 2, 3)
        return (
            jnp.where(same[None, :, None, :, None], weight[:, :, :, None, :], 0.0)
            .reshape(plane * cap, lines * rows)
            .astype(jnp.bfloat16)
        )

    weight_hi = spread(weight_hi)
    weight_lo = spread(weight_lo)
    line_flat = line.reshape(lines * padded, width)
    half = width // 2
    gate_up = dequant(w_in[0], scale_in[0])
    down_proj = dequant(w_out[0], scale_out[0])
    hidden_width = down_proj.shape[0]
    group = ("dp", "expert")

    def send(part):
        moved = lax.all_to_all(
            part.reshape(plane, cap, part.shape[1]), group, split_axis=0, concat_axis=0, tiled=True
        )
        return moved.reshape(plane * cap, part.shape[1])

    blocks = [
        send(
            jnp.dot(
                select_full, line_flat[:, h * half : (h + 1) * half], preferred_element_type=jnp.float32
            ).astype(jnp.bfloat16)
        )
        for h in range(2)
    ]
    mixed_in = jnp.dot(blocks[0], gate_up[:half], preferred_element_type=jnp.float32) + jnp.dot(
        blocks[1], gate_up[half:], preferred_element_type=jnp.float32
    )
    hidden = (jax.nn.silu(mixed_in[:, :hidden_width]) * mixed_in[:, hidden_width:]).astype(
        jnp.bfloat16
    )
    contract = (((0,), (0,)), ((), ()))
    mixed_parts = []
    for h in range(2):
        output = jnp.dot(
            hidden, down_proj[:, h * half : (h + 1) * half], preferred_element_type=jnp.float32
        ).astype(jnp.bfloat16)
        back = send(output)
        partial = lax.dot_general(
            weight_hi, back, contract, preferred_element_type=jnp.float32
        ) + lax.dot_general(weight_lo, back, contract, preferred_element_type=jnp.float32)
        combined = lax.psum_scatter(partial, "tensor", scatter_dimension=0, tiled=True)
        mixed_parts.append((x_float[:, h * half : (h + 1) * half] + combined).astype(jnp.bfloat16))
    mixed = jnp.concatenate(mixed_parts, axis=1)

    local_sync = w_sync.reshape(width, -1)
    proj = sum(
        jnp.dot(
            lax.all_gather(mixed_parts[h], "tensor", axis=0, tiled=True),
            local_sync[h * half : (h + 1) * half],
            preferred_element_type=jnp.float32,
        )
        for h in range(2)
    ).astype(jnp.bfloat16)
    half = proj.shape[1] // 2
    heads_here = head_weight.shape[0]
    head_size = half // heads_here
    frames = frame_rows.shape[2]
    clip_len = proj.shape[0]
    clip_index = jnp.arange(clip_len, dtype=jnp.int32)
    pick_audio = (frame_rows[0, 0][:, None] == clip_index[None, :]).astype(jnp.bfloat16)
    pick_video = (frame_rows[0, 1][:, None] == clip_index[None, :]).astype(jnp.bfloat16)
    audio = (
        jnp.dot(pick_audio, proj[:, :half], preferred_element_type=jnp.float32)
        .astype(jnp.bfloat16)
        .reshape(frames, heads_here, head_size)
    )
    video = (
        jnp.dot(pick_video, proj[:, half:], preferred_element_type=jnp.float32)
        .astype(jnp.bfloat16)
        .reshape(frames, heads_here, head_size)
    )
    grams = jnp.einsum("thd,shd->hts", audio, video, preferred_element_type=jnp.float32)
    times = jnp.arange(frames, dtype=jnp.int32)
    offsets = times[None, :] - times[:, None]
    diagonal = (
        (offsets[None, :, :] == lag_offsets[:, None, None])
        .astype(jnp.float32)
        .reshape(lag_offsets.shape[0], frames * frames)
    )
    sums = lax.dot_general(
        grams.reshape(heads_here, frames * frames),
        diagonal,
        (((1,), (1,)), ((), ())),
        precision=lax.Precision.HIGHEST,
        preferred_element_type=jnp.float32,
    )
    counts = (frames - jnp.abs(lag_offsets)).astype(jnp.float32)
    score = sums / jnp.sqrt(counts * head_size)[None, :]
    partial_logits = jnp.sum(head_weight[:, None] * score, axis=0)
    sync_logits = lax.psum(partial_logits, "tensor")
    return (mixed, sync_logits[None, :])


def solution(mesh):
    return jax.shard_map(
        shards,
        mesh=mesh,
        in_specs=(
            P(("dp", "expert", "tensor"), None),
            P(),
            P(("dp", "expert", "tensor"), None),
            P(("dp", "expert", "tensor"), None),
            P(("dp", "expert", "tensor"), None, None),
            P(("dp", "expert", "tensor"), None, None),
            P(("dp", "expert", "tensor"), None, None),
            P(("dp", "expert", "tensor"), None, None),
            P(None, None, "tensor"),
            P("tensor"),
            P(("dp", "expert"), None, None),
            P(),
        ),
        out_specs=(P(("dp", "expert", "tensor"), None), P(("dp", "expert"), None)),
        check_vma=False,
    )
```

```python
import jax
import jax.numpy as jnp
from jax import lax
from jax.sharding import PartitionSpec as P


def dequant(weights, scales):
    block = weights.shape[0] // scales.shape[0]
    full = jnp.repeat(jnp.repeat(scales, block, axis=0), block, axis=1)
    return (weights.astype(jnp.float32) * full).astype(jnp.bfloat16)


def shards(
    tokens,
    norm_gain,
    expert_ids,
    gate_weights,
    w_in,
    scale_in,
    w_out,
    scale_out,
    w_sync,
    head_weight,
    frame_rows,
    lag_offsets,
):
    rows, width = tokens.shape
    top = expert_ids.shape[1]
    lines = lax.axis_size("tensor")
    plane = lax.axis_size(("dp", "expert"))
    experts_all = plane * lines * w_in.shape[0]
    most = 2 * rows * top // experts_all
    cap = lines * most
    here = lax.axis_index("tensor")
    x_float = tokens.astype(jnp.float32)
    normed = (
        x_float * lax.rsqrt(jnp.mean(x_float * x_float, axis=-1, keepdims=True) + 1e-06) * norm_gain
    ).astype(jnp.bfloat16)

    flat_ids = expert_ids.reshape(-1)
    pair_count = rows * top
    onehot = (flat_ids[:, None] == jnp.arange(experts_all, dtype=jnp.int32)[None, :]).astype(
        jnp.bfloat16
    )
    pair_index = jnp.arange(pair_count, dtype=jnp.int32)
    earlier = (pair_index[None, :] < pair_index[:, None]).astype(jnp.bfloat16)
    before = jnp.dot(earlier, onehot, preferred_element_type=jnp.float32)
    slots = jnp.sum(before * onehot.astype(jnp.float32), axis=1).reshape(rows, top)
    gate = gate_weights.astype(jnp.float32)
    gate_top = lax.reduce_precision(gate, exponent_bits=8, mantissa_bits=7)
    routing = jnp.concatenate(
        [
            expert_ids.astype(jnp.bfloat16),
            slots.astype(jnp.bfloat16),
            gate_top.astype(jnp.bfloat16),
            (gate - gate_top).astype(jnp.bfloat16),
        ],
        axis=1,
    )
    half = width // 2
    extra = rows * 4 * top // half
    padded = rows + 16
    packed = jnp.concatenate(
        [
            normed[:, :half],
            routing.reshape(extra, half),
            jnp.zeros((padded - rows - extra, half), jnp.bfloat16),
        ],
        axis=0,
    )
    line_a = lax.all_gather(packed, "tensor", axis=0, tiled=False)
    line_b = lax.all_gather(normed[:, half:], "tensor", axis=0, tiled=False)
    line_routing = line_a[:, rows : rows + extra, :].reshape(lines, rows, 4 * top)
    ids_l = line_routing[:, :, :top].astype(jnp.int32)
    slot_l = line_routing[:, :, top : 2 * top].astype(jnp.int32)
    gate_hi = line_routing[:, :, 2 * top : 3 * top].astype(jnp.float32)
    gate_lo = line_routing[:, :, 3 * top :].astype(jnp.float32)
    mine = (ids_l % lines) == here
    target = jnp.where(mine, (ids_l // lines) * most + slot_l, -1)
    slot_ids = jnp.arange(plane * most, dtype=jnp.int32)
    match = target[:, None, :, :] == slot_ids[None, :, None, None]
    select = jnp.any(match, axis=3)
    weight_hi = jnp.sum(jnp.where(match, gate_hi[:, None, :, :], 0.0), axis=3)
    weight_lo = jnp.sum(jnp.where(match, gate_lo[:, None, :, :], 0.0), axis=3)
    same = (
        jnp.arange(lines, dtype=jnp.int32)[:, None] == jnp.arange(lines, dtype=jnp.int32)[None, :]
    )
    select = select.reshape(lines, plane, most, rows).transpose(1, 0, 2, 3)
    select_full = (
        (select[:, :, :, None, :] & same[None, :, None, :, None])
        .reshape(plane * cap, lines * rows)
        .astype(jnp.bfloat16)
    )
    select_pad = jnp.pad(
        select_full.reshape(plane * cap, lines, rows), ((0, 0), (0, 0), (0, padded - rows))
    ).reshape(plane * cap, lines * padded)

    def spread(weight):
        weight = weight.reshape(lines, plane, most, rows).transpose(1, 0, 2, 3)
        return (
            jnp.where(same[None, :, None, :, None], weight[:, :, :, None, :], 0.0)
            .reshape(plane * cap, lines * rows)
            .astype(jnp.bfloat16)
        )

    weight_hi = spread(weight_hi)
    weight_lo = spread(weight_lo)
    line_parts = [line_a.reshape(lines * padded, half), line_b.reshape(lines * rows, half)]
    select_parts = [select_pad, select_full]
    gate_up = dequant(w_in[0], scale_in[0])
    down_proj = dequant(w_out[0], scale_out[0])
    hidden_width = down_proj.shape[0]
    group = ("dp", "expert")

    def send(part):
        moved = lax.all_to_all(
            part.reshape(plane, cap, part.shape[1]), group, split_axis=0, concat_axis=0, tiled=True
        )
        return moved.reshape(plane * cap, part.shape[1])

    blocks = [
        send(
            jnp.dot(
                select_parts[h], line_parts[h], preferred_element_type=jnp.float32
            ).astype(jnp.bfloat16)
        )
        for h in range(2)
    ]
    mixed_in = jnp.dot(blocks[0], gate_up[:half], preferred_element_type=jnp.float32) + jnp.dot(
        blocks[1], gate_up[half:], preferred_element_type=jnp.float32
    )
    hidden = (jax.nn.silu(mixed_in[:, :hidden_width]) * mixed_in[:, hidden_width:]).astype(
        jnp.bfloat16
    )
    contract = (((0,), (0,)), ((), ()))
    mixed_parts = []
    for h in range(2):
        output = jnp.dot(
            hidden, down_proj[:, h * half : (h + 1) * half], preferred_element_type=jnp.float32
        ).astype(jnp.bfloat16)
        back = send(output)
        partial = lax.dot_general(
            weight_hi, back, contract, preferred_element_type=jnp.float32
        ) + lax.dot_general(weight_lo, back, contract, preferred_element_type=jnp.float32)
        combined = lax.psum_scatter(partial, "tensor", scatter_dimension=0, tiled=True)
        mixed_parts.append((x_float[:, h * half : (h + 1) * half] + combined).astype(jnp.bfloat16))
    mixed = jnp.concatenate(mixed_parts, axis=1)

    local_sync = w_sync.reshape(width, -1)
    proj = sum(
        jnp.dot(
            lax.all_gather(mixed_parts[h], "tensor", axis=0, tiled=True),
            local_sync[h * half : (h + 1) * half],
            preferred_element_type=jnp.float32,
        )
        for h in range(2)
    ).astype(jnp.bfloat16)
    half = proj.shape[1] // 2
    heads_here = head_weight.shape[0]
    head_size = half // heads_here
    frames = frame_rows.shape[2]
    clip_len = proj.shape[0]
    clip_index = jnp.arange(clip_len, dtype=jnp.int32)
    pick_audio = (frame_rows[0, 0][:, None] == clip_index[None, :]).astype(jnp.bfloat16)
    pick_video = (frame_rows[0, 1][:, None] == clip_index[None, :]).astype(jnp.bfloat16)
    audio = (
        jnp.dot(pick_audio, proj[:, :half], preferred_element_type=jnp.float32)
        .astype(jnp.bfloat16)
        .reshape(frames, heads_here, head_size)
    )
    video = (
        jnp.dot(pick_video, proj[:, half:], preferred_element_type=jnp.float32)
        .astype(jnp.bfloat16)
        .reshape(frames, heads_here, head_size)
    )
    grams = jnp.einsum("thd,shd->hts", audio, video, preferred_element_type=jnp.float32)
    times = jnp.arange(frames, dtype=jnp.int32)
    offsets = times[None, :] - times[:, None]
    diagonal = (
        (offsets[None, :, :] == lag_offsets[:, None, None])
        .astype(jnp.float32)
        .reshape(lag_offsets.shape[0], frames * frames)
    )
    sums = lax.dot_general(
        grams.reshape(heads_here, frames * frames),
        diagonal,
        (((1,), (1,)), ((), ())),
        precision=lax.Precision.HIGHEST,
        preferred_element_type=jnp.float32,
    )
    counts = (frames - jnp.abs(lag_offsets)).astype(jnp.float32)
    score = sums / jnp.sqrt(counts * head_size)[None, :]
    partial_logits = jnp.sum(head_weight[:, None] * score, axis=0)
    sync_logits = lax.psum(partial_logits, "tensor")
    return (mixed, sync_logits[None, :])


def solution(mesh):
    return jax.shard_map(
        shards,
        mesh=mesh,
        in_specs=(
            P(("dp", "expert", "tensor"), None),
            P(),
            P(("dp", "expert", "tensor"), None),
            P(("dp", "expert", "tensor"), None),
            P(("dp", "expert", "tensor"), None, None),
            P(("dp", "expert", "tensor"), None, None),
            P(("dp", "expert", "tensor"), None, None),
            P(("dp", "expert", "tensor"), None, None),
            P(None, None, "tensor"),
            P("tensor"),
            P(("dp", "expert"), None, None),
            P(),
        ),
        out_specs=(P(("dp", "expert", "tensor"), None), P(("dp", "expert"), None)),
        check_vma=False,
    )
```

```python
import jax
import jax.numpy as jnp
from jax import lax
from jax.sharding import PartitionSpec as P


def dequant(weights, scales):
    block = weights.shape[0] // scales.shape[0]
    full = jnp.repeat(jnp.repeat(scales, block, axis=0), block, axis=1)
    return (weights.astype(jnp.float32) * full).astype(jnp.bfloat16)


def shards(
    tokens,
    norm_gain,
    expert_ids,
    gate_weights,
    w_in,
    scale_in,
    w_out,
    scale_out,
    w_sync,
    head_weight,
    frame_rows,
    lag_offsets,
):
    rows, width = tokens.shape
    top = expert_ids.shape[1]
    lines = lax.axis_size("tensor")
    plane = lax.axis_size(("dp", "expert"))
    experts_all = plane * lines * w_in.shape[0]
    most = 2 * rows * top // experts_all
    cap = lines * most
    here = lax.axis_index("tensor")
    x_float = tokens.astype(jnp.float32)
    normed = (
        x_float * lax.rsqrt(jnp.mean(x_float * x_float, axis=-1, keepdims=True) + 1e-06) * norm_gain
    ).astype(jnp.bfloat16)

    flat_ids = expert_ids.reshape(-1)
    pair_count = rows * top
    onehot = (flat_ids[:, None] == jnp.arange(experts_all, dtype=jnp.int32)[None, :]).astype(
        jnp.bfloat16
    )
    pair_index = jnp.arange(pair_count, dtype=jnp.int32)
    earlier = (pair_index[None, :] < pair_index[:, None]).astype(jnp.bfloat16)
    before = jnp.dot(earlier, onehot, preferred_element_type=jnp.float32)
    slots = jnp.sum(before * onehot.astype(jnp.float32), axis=1).reshape(rows, top)
    gate = gate_weights.astype(jnp.float32)
    gate_top = lax.reduce_precision(gate, exponent_bits=8, mantissa_bits=7)
    routing = jnp.concatenate(
        [
            expert_ids.astype(jnp.bfloat16),
            slots.astype(jnp.bfloat16),
            gate_top.astype(jnp.bfloat16),
            (gate - gate_top).astype(jnp.bfloat16),
        ],
        axis=1,
    )
    half = width // 2
    extra = rows * 4 * top // half
    padded = rows + 16
    packed = jnp.concatenate(
        [
            normed[:, :half],
            routing.reshape(extra, half),
            jnp.zeros((padded - rows - extra, half), jnp.bfloat16),
        ],
        axis=0,
    )
    line_a = lax.all_gather(packed, "tensor", axis=0, tiled=False)
    line_b = lax.all_gather(normed[:, half:], "tensor", axis=0, tiled=False)
    line_routing = line_a[:, rows : rows + extra, :].reshape(lines, rows, 4 * top)
    ids_l = line_routing[:, :, :top].astype(jnp.int32)
    slot_l = line_routing[:, :, top : 2 * top].astype(jnp.int32)
    gate_hi = line_routing[:, :, 2 * top : 3 * top].astype(jnp.float32)
    gate_lo = line_routing[:, :, 3 * top :].astype(jnp.float32)
    mine = (ids_l % lines) == here
    target = jnp.where(mine, (ids_l // lines) * most + slot_l, -1)
    slot_ids = jnp.arange(plane * most, dtype=jnp.int32)
    match = target[:, None, :, :] == slot_ids[None, :, None, None]
    select = jnp.any(match, axis=3)
    weight_hi = jnp.sum(jnp.where(match, gate_hi[:, None, :, :], 0.0), axis=3)
    weight_lo = jnp.sum(jnp.where(match, gate_lo[:, None, :, :], 0.0), axis=3)
    select = select.astype(jnp.bfloat16).reshape(lines, plane, most, rows)
    select_pad = jnp.pad(select, ((0, 0), (0, 0), (0, 0), (0, padded - rows)))
    weight_hi = weight_hi.astype(jnp.bfloat16).reshape(lines, plane, most, rows)
    weight_lo = weight_lo.astype(jnp.bfloat16).reshape(lines, plane, most, rows)
    line_parts = [line_a, line_b]
    select_parts = [select_pad, select]
    gate_up = dequant(w_in[0], scale_in[0])
    down_proj = dequant(w_out[0], scale_out[0])
    hidden_width = down_proj.shape[0]
    group = ("dp", "expert")

    def send(part):
        moved = lax.all_to_all(
            part.reshape(plane, cap, part.shape[1]), group, split_axis=0, concat_axis=0, tiled=True
        )
        return moved.reshape(plane * cap, part.shape[1])

    blocks = [
        send(
            jnp.einsum(
                "bpsr,brd->pbsd", select_parts[h], line_parts[h], preferred_element_type=jnp.float32
            )
            .astype(jnp.bfloat16)
            .reshape(plane * cap, half)
        )
        for h in range(2)
    ]
    mixed_in = jnp.dot(blocks[0], gate_up[:half], preferred_element_type=jnp.float32) + jnp.dot(
        blocks[1], gate_up[half:], preferred_element_type=jnp.float32
    )
    hidden = (jax.nn.silu(mixed_in[:, :hidden_width]) * mixed_in[:, hidden_width:]).astype(
        jnp.bfloat16
    )
    mixed_parts = []
    for h in range(2):
        output = jnp.dot(
            hidden, down_proj[:, h * half : (h + 1) * half], preferred_element_type=jnp.float32
        ).astype(jnp.bfloat16)
        back = send(output)
        back = back.reshape(plane, lines, most, half)
        partial = jnp.einsum(
            "bpsr,pbsd->brd", weight_hi, back, preferred_element_type=jnp.float32
        ) + jnp.einsum("bpsr,pbsd->brd", weight_lo, back, preferred_element_type=jnp.float32)
        combined = lax.psum_scatter(
            partial.reshape(lines * rows, half), "tensor", scatter_dimension=0, tiled=True
        )
        mixed_parts.append(x_float[:, h * half : (h + 1) * half] + combined)
    mixed = jnp.concatenate(mixed_parts, axis=1).astype(jnp.bfloat16)

    local_sync = w_sync.reshape(width, -1)
    proj = jnp.dot(
        lax.all_gather(mixed, "tensor", axis=0, tiled=True),
        local_sync,
        preferred_element_type=jnp.float32,
    ).astype(jnp.bfloat16)
    half = proj.shape[1] // 2
    heads_here = head_weight.shape[0]
    head_size = half // heads_here
    frames = frame_rows.shape[2]
    clip_len = proj.shape[0]
    clip_index = jnp.arange(clip_len, dtype=jnp.int32)
    pick_audio = (frame_rows[0, 0][:, None] == clip_index[None, :]).astype(jnp.bfloat16)
    pick_video = (frame_rows[0, 1][:, None] == clip_index[None, :]).astype(jnp.bfloat16)
    audio = (
        jnp.dot(pick_audio, proj[:, :half], preferred_element_type=jnp.float32)
        .astype(jnp.bfloat16)
        .reshape(frames, heads_here, head_size)
    )
    video = (
        jnp.dot(pick_video, proj[:, half:], preferred_element_type=jnp.float32)
        .astype(jnp.bfloat16)
        .reshape(frames, heads_here, head_size)
    )
    grams = jnp.einsum("thd,shd->hts", audio, video, preferred_element_type=jnp.float32)
    times = jnp.arange(frames, dtype=jnp.int32)
    offsets = times[None, :] - times[:, None]
    diagonal = (
        (offsets[None, :, :] == lag_offsets[:, None, None])
        .astype(jnp.float32)
        .reshape(lag_offsets.shape[0], frames * frames)
    )
    sums = lax.dot_general(
        grams.reshape(heads_here, frames * frames),
        diagonal,
        (((1,), (1,)), ((), ())),
        precision=lax.Precision.HIGHEST,
        preferred_element_type=jnp.float32,
    )
    counts = (frames - jnp.abs(lag_offsets)).astype(jnp.float32)
    score = sums / jnp.sqrt(counts * head_size)[None, :]
    partial_logits = jnp.sum(head_weight[:, None] * score, axis=0)
    sync_logits = lax.psum(partial_logits, "tensor")
    return (mixed, sync_logits[None, :])


def solution(mesh):
    return jax.shard_map(
        shards,
        mesh=mesh,
        in_specs=(
            P(("dp", "expert", "tensor"), None),
            P(),
            P(("dp", "expert", "tensor"), None),
            P(("dp", "expert", "tensor"), None),
            P(("dp", "expert", "tensor"), None, None),
            P(("dp", "expert", "tensor"), None, None),
            P(("dp", "expert", "tensor"), None, None),
            P(("dp", "expert", "tensor"), None, None),
            P(None, None, "tensor"),
            P("tensor"),
            P(("dp", "expert"), None, None),
            P(),
        ),
        out_specs=(P(("dp", "expert", "tensor"), None), P(("dp", "expert"), None)),
        check_vma=False,
    )
```

```python
import jax
import jax.numpy as jnp
from jax import lax
from jax.sharding import PartitionSpec as P


def dequant(weights, scales):
    block = weights.shape[0] // scales.shape[0]
    full = jnp.repeat(jnp.repeat(scales, block, axis=0), block, axis=1)
    return (weights.astype(jnp.float32) * full).astype(jnp.bfloat16)


def shards(
    tokens,
    norm_gain,
    expert_ids,
    gate_weights,
    w_in,
    scale_in,
    w_out,
    scale_out,
    w_sync,
    head_weight,
    frame_rows,
    lag_offsets,
):
    rows, width = tokens.shape
    top = expert_ids.shape[1]
    lines = lax.axis_size("tensor")
    plane = lax.axis_size(("dp", "expert"))
    experts_all = plane * lines * w_in.shape[0]
    most = 2 * rows * top // experts_all
    cap = lines * most
    here = lax.axis_index("tensor")
    x_float = tokens.astype(jnp.float32)
    normed = (
        x_float * lax.rsqrt(jnp.mean(x_float * x_float, axis=-1, keepdims=True) + 1e-06) * norm_gain
    ).astype(jnp.bfloat16)

    flat_ids = expert_ids.reshape(-1)
    pair_count = rows * top
    onehot = (flat_ids[:, None] == jnp.arange(experts_all, dtype=jnp.int32)[None, :]).astype(
        jnp.bfloat16
    )
    pair_index = jnp.arange(pair_count, dtype=jnp.int32)
    earlier = (pair_index[None, :] < pair_index[:, None]).astype(jnp.bfloat16)
    before = jnp.dot(earlier, onehot, preferred_element_type=jnp.float32)
    slots = jnp.sum(before * onehot.astype(jnp.float32), axis=1).reshape(rows, top)
    gate = gate_weights.astype(jnp.float32)
    gate_top = lax.reduce_precision(gate, exponent_bits=8, mantissa_bits=7)
    routing = jnp.concatenate(
        [
            expert_ids.astype(jnp.bfloat16),
            slots.astype(jnp.bfloat16),
            gate_top.astype(jnp.bfloat16),
            (gate - gate_top).astype(jnp.bfloat16),
        ],
        axis=1,
    )
    half = width // 2
    extra = rows * 4 * top // half
    padded = rows + 16
    packed = jnp.concatenate(
        [
            normed[:, :half],
            routing.reshape(extra, half),
            jnp.zeros((padded - rows - extra, half), jnp.bfloat16),
        ],
        axis=0,
    )
    line_a = lax.all_gather(packed, "tensor", axis=0, tiled=False)
    line_b = lax.all_to_all(
        jnp.broadcast_to(normed[None, :, half:], (lines, rows, half)),
        "tensor",
        split_axis=0,
        concat_axis=0,
        tiled=True,
    )
    line_routing = line_a[:, rows : rows + extra, :].reshape(lines, rows, 4 * top)
    ids_l = line_routing[:, :, :top].astype(jnp.int32)
    slot_l = line_routing[:, :, top : 2 * top].astype(jnp.int32)
    gate_hi = line_routing[:, :, 2 * top : 3 * top].astype(jnp.float32)
    gate_lo = line_routing[:, :, 3 * top :].astype(jnp.float32)
    mine = (ids_l % lines) == here
    target = jnp.where(mine, (ids_l // lines) * most + slot_l, -1)
    slot_ids = jnp.arange(plane * most, dtype=jnp.int32)
    match = target[:, None, :, :] == slot_ids[None, :, None, None]
    select = jnp.any(match, axis=3)
    weight_hi = jnp.sum(jnp.where(match, gate_hi[:, None, :, :], 0.0), axis=3)
    weight_lo = jnp.sum(jnp.where(match, gate_lo[:, None, :, :], 0.0), axis=3)
    select = select.astype(jnp.bfloat16).reshape(lines, plane, most, rows)
    select_pad = jnp.pad(select, ((0, 0), (0, 0), (0, 0), (0, padded - rows)))
    weight_hi = weight_hi.astype(jnp.bfloat16).reshape(lines, plane, most, rows)
    weight_lo = weight_lo.astype(jnp.bfloat16).reshape(lines, plane, most, rows)
    line_parts = [line_a, line_b]
    select_parts = [select_pad, select]
    gate_up = dequant(w_in[0], scale_in[0])
    down_proj = dequant(w_out[0], scale_out[0])
    hidden_width = down_proj.shape[0]
    group = ("dp", "expert")

    def send(part):
        moved = lax.all_to_all(
            part.reshape(plane, cap, part.shape[1]), group, split_axis=0, concat_axis=0, tiled=True
        )
        return moved.reshape(plane * cap, part.shape[1])

    blocks = [
        send(
            jnp.einsum(
                "bpsr,brd->pbsd", select_parts[h], line_parts[h], preferred_element_type=jnp.float32
            )
            .astype(jnp.bfloat16)
            .reshape(plane * cap, half)
        )
        for h in range(2)
    ]
    mixed_in = jnp.dot(blocks[0], gate_up[:half], preferred_element_type=jnp.float32) + jnp.dot(
        blocks[1], gate_up[half:], preferred_element_type=jnp.float32
    )
    hidden = (jax.nn.silu(mixed_in[:, :hidden_width]) * mixed_in[:, hidden_width:]).astype(
        jnp.bfloat16
    )
    mixed_parts = []
    for h in range(2):
        output = jnp.dot(
            hidden, down_proj[:, h * half : (h + 1) * half], preferred_element_type=jnp.float32
        ).astype(jnp.bfloat16)
        back = send(output)
        back = back.reshape(plane, lines, most, half)
        partial = jnp.einsum(
            "bpsr,pbsd->brd", weight_hi, back, preferred_element_type=jnp.float32
        ) + jnp.einsum("bpsr,pbsd->brd", weight_lo, back, preferred_element_type=jnp.float32)
        if h == 0:
            combined = lax.psum_scatter(
                partial.reshape(lines * rows, half), "tensor", scatter_dimension=0, tiled=True
            )
        else:
            combined = jnp.sum(
                lax.all_to_all(partial, "tensor", split_axis=0, concat_axis=0, tiled=True), axis=0
            )
        mixed_parts.append(x_float[:, h * half : (h + 1) * half] + combined)
    mixed = jnp.concatenate(mixed_parts, axis=1).astype(jnp.bfloat16)

    local_sync = w_sync.reshape(width, -1)
    proj = jnp.dot(
        lax.all_gather(mixed, "tensor", axis=0, tiled=True),
        local_sync,
        preferred_element_type=jnp.float32,
    ).astype(jnp.bfloat16)
    half = proj.shape[1] // 2
    heads_here = head_weight.shape[0]
    head_size = half // heads_here
    frames = frame_rows.shape[2]
    clip_len = proj.shape[0]
    clip_index = jnp.arange(clip_len, dtype=jnp.int32)
    pick_audio = (frame_rows[0, 0][:, None] == clip_index[None, :]).astype(jnp.bfloat16)
    pick_video = (frame_rows[0, 1][:, None] == clip_index[None, :]).astype(jnp.bfloat16)
    audio = (
        jnp.dot(pick_audio, proj[:, :half], preferred_element_type=jnp.float32)
        .astype(jnp.bfloat16)
        .reshape(frames, heads_here, head_size)
    )
    video = (
        jnp.dot(pick_video, proj[:, half:], preferred_element_type=jnp.float32)
        .astype(jnp.bfloat16)
        .reshape(frames, heads_here, head_size)
    )
    grams = jnp.einsum("thd,shd->hts", audio, video, preferred_element_type=jnp.float32)
    times = jnp.arange(frames, dtype=jnp.int32)
    offsets = times[None, :] - times[:, None]
    diagonal = (
        (offsets[None, :, :] == lag_offsets[:, None, None])
        .astype(jnp.float32)
        .reshape(lag_offsets.shape[0], frames * frames)
    )
    sums = lax.dot_general(
        grams.reshape(heads_here, frames * frames),
        diagonal,
        (((1,), (1,)), ((), ())),
        precision=lax.Precision.HIGHEST,
        preferred_element_type=jnp.float32,
    )
    counts = (frames - jnp.abs(lag_offsets)).astype(jnp.float32)
    score = sums / jnp.sqrt(counts * head_size)[None, :]
    partial_logits = jnp.sum(head_weight[:, None] * score, axis=0)
    sync_logits = lax.psum(partial_logits, "tensor")
    return (mixed, sync_logits[None, :])


def solution(mesh):
    return jax.shard_map(
        shards,
        mesh=mesh,
        in_specs=(
            P(("dp", "expert", "tensor"), None),
            P(),
            P(("dp", "expert", "tensor"), None),
            P(("dp", "expert", "tensor"), None),
            P(("dp", "expert", "tensor"), None, None),
            P(("dp", "expert", "tensor"), None, None),
            P(("dp", "expert", "tensor"), None, None),
            P(("dp", "expert", "tensor"), None, None),
            P(None, None, "tensor"),
            P("tensor"),
            P(("dp", "expert"), None, None),
            P(),
        ),
        out_specs=(P(("dp", "expert", "tensor"), None), P(("dp", "expert"), None)),
        check_vma=False,
    )
```

```python
import jax
import jax.numpy as jnp
from jax import lax
from jax.sharding import PartitionSpec as P


def dequant(weights, scales):
    block = weights.shape[0] // scales.shape[0]
    full = jnp.repeat(jnp.repeat(scales, block, axis=0), block, axis=1)
    return (weights.astype(jnp.float32) * full).astype(jnp.bfloat16)


def shards(
    tokens,
    norm_gain,
    expert_ids,
    gate_weights,
    w_in,
    scale_in,
    w_out,
    scale_out,
    w_sync,
    head_weight,
    frame_rows,
    lag_offsets,
):
    rows, width = tokens.shape
    top = expert_ids.shape[1]
    lines = lax.axis_size("tensor")
    plane = lax.axis_size(("dp", "expert"))
    experts_all = plane * lines * w_in.shape[0]
    most = 2 * rows * top // experts_all
    cap = lines * most
    here = lax.axis_index("tensor")
    x_float = tokens.astype(jnp.float32)
    normed = (
        x_float * lax.rsqrt(jnp.mean(x_float * x_float, axis=-1, keepdims=True) + 1e-06) * norm_gain
    ).astype(jnp.bfloat16)

    flat_ids = expert_ids.reshape(-1)
    pair_count = rows * top
    onehot = (flat_ids[:, None] == jnp.arange(experts_all, dtype=jnp.int32)[None, :]).astype(
        jnp.bfloat16
    )
    pair_index = jnp.arange(pair_count, dtype=jnp.int32)
    earlier = (pair_index[None, :] < pair_index[:, None]).astype(jnp.bfloat16)
    before = jnp.dot(earlier, onehot, preferred_element_type=jnp.float32)
    slots = jnp.sum(before * onehot.astype(jnp.float32), axis=1).reshape(rows, top)
    gate = gate_weights.astype(jnp.float32)
    gate_top = lax.reduce_precision(gate, exponent_bits=8, mantissa_bits=7)
    routing = jnp.concatenate(
        [
            expert_ids.astype(jnp.bfloat16),
            slots.astype(jnp.bfloat16),
            gate_top.astype(jnp.bfloat16),
            (gate - gate_top).astype(jnp.bfloat16),
        ],
        axis=1,
    )
    half = width // 2
    extra = rows * 4 * top // half
    padded = rows + 16
    packed = jnp.concatenate(
        [
            normed[:, :half],
            routing.reshape(extra, half),
            jnp.zeros((padded - rows - extra, half), jnp.bfloat16),
        ],
        axis=0,
    )
    line_a = lax.all_gather(packed, "tensor", axis=0, tiled=False)
    line_b = lax.all_gather(normed[:, half:], "tensor", axis=0, tiled=False)
    line_routing = line_a[:, rows : rows + extra, :].reshape(lines, rows, 4 * top)
    ids_l = line_routing[:, :, :top].astype(jnp.int32)
    slot_l = line_routing[:, :, top : 2 * top].astype(jnp.int32)
    gate_hi = line_routing[:, :, 2 * top : 3 * top].astype(jnp.float32)
    gate_lo = line_routing[:, :, 3 * top :].astype(jnp.float32)
    mine = (ids_l % lines) == here
    target = jnp.where(mine, (ids_l // lines) * most + slot_l, -1)
    slot_ids = jnp.arange(plane * most, dtype=jnp.int32)
    match = target[:, None, :, :] == slot_ids[None, :, None, None]
    select = jnp.any(match, axis=3)
    weight_hi = jnp.sum(jnp.where(match, gate_hi[:, None, :, :], 0.0), axis=3)
    weight_lo = jnp.sum(jnp.where(match, gate_lo[:, None, :, :], 0.0), axis=3)
    select = select.astype(jnp.bfloat16).reshape(lines, plane, most, rows)
    select_pad = jnp.pad(select, ((0, 0), (0, 0), (0, 0), (0, padded - rows)))
    weight_hi = weight_hi.astype(jnp.bfloat16).reshape(lines, plane, most, rows)
    weight_lo = weight_lo.astype(jnp.bfloat16).reshape(lines, plane, most, rows)
    line_parts = [line_a, line_b]
    select_parts = [select_pad, select]
    gate_up = dequant(w_in[0], scale_in[0])
    down_proj = dequant(w_out[0], scale_out[0])
    hidden_width = down_proj.shape[0]
    group = ("dp", "expert")

    def send(part):
        moved = lax.all_to_all(
            part.reshape(plane, cap, part.shape[1]), group, split_axis=0, concat_axis=0, tiled=True
        )
        return moved.reshape(plane * cap, part.shape[1])

    blocks = [
        send(
            jnp.einsum(
                "bpsr,brd->pbsd", select_parts[h], line_parts[h], preferred_element_type=jnp.float32
            )
            .astype(jnp.bfloat16)
            .reshape(plane * cap, half)
        )
        for h in range(2)
    ]
    mixed_in = jnp.dot(blocks[0], gate_up[:half], preferred_element_type=jnp.float32) + jnp.dot(
        blocks[1], gate_up[half:], preferred_element_type=jnp.float32
    )
    hidden = (jax.nn.silu(mixed_in[:, :hidden_width]) * mixed_in[:, hidden_width:]).astype(
        jnp.bfloat16
    )
    mixed_parts = []
    for h in range(2):
        output = jnp.dot(
            hidden, down_proj[:, h * half : (h + 1) * half], preferred_element_type=jnp.float32
        ).astype(jnp.bfloat16)
        back = send(output)
        back = back.reshape(plane, lines, most, half)
        partial = jnp.einsum(
            "bpsr,pbsd->brd", weight_hi, back, preferred_element_type=jnp.float32
        ) + jnp.einsum("bpsr,pbsd->brd", weight_lo, back, preferred_element_type=jnp.float32)
        combined = lax.psum_scatter(
            partial.reshape(lines * rows, half), "tensor", scatter_dimension=0, tiled=True
        )
        mixed_parts.append(x_float[:, h * half : (h + 1) * half] + combined)
    mixed = jnp.concatenate(mixed_parts, axis=1).astype(jnp.bfloat16)

    local_sync = w_sync.reshape(width, -1)
    proj = jnp.dot(
        lax.all_gather(mixed, "tensor", axis=0, tiled=True),
        local_sync,
        preferred_element_type=jnp.float32,
    ).astype(jnp.bfloat16)
    half = proj.shape[1] // 2
    heads_here = head_weight.shape[0]
    head_size = half // heads_here
    frames = frame_rows.shape[2]
    clip_len = proj.shape[0]
    clip_index = jnp.arange(clip_len, dtype=jnp.int32)
    pick_audio = (frame_rows[0, 0][:, None] == clip_index[None, :]).astype(jnp.bfloat16)
    pick_video = (frame_rows[0, 1][:, None] == clip_index[None, :]).astype(jnp.bfloat16)
    audio = (
        jnp.dot(pick_audio, proj[:, :half], preferred_element_type=jnp.float32)
        .astype(jnp.bfloat16)
        .reshape(frames, heads_here, head_size)
    )
    video = (
        jnp.dot(pick_video, proj[:, half:], preferred_element_type=jnp.float32)
        .astype(jnp.bfloat16)
        .reshape(frames, heads_here, head_size)
    )
    grams = jnp.einsum("thd,shd->hts", audio, video, preferred_element_type=jnp.float32)
    times = jnp.arange(frames, dtype=jnp.int32)
    offsets = times[None, :] - times[:, None]
    diagonal = (
        (offsets[None, :, :] == lag_offsets[:, None, None])
        .astype(jnp.float32)
        .reshape(lag_offsets.shape[0], frames * frames)
    )
    sums = lax.dot_general(
        grams.reshape(heads_here, frames * frames),
        diagonal,
        (((1,), (1,)), ((), ())),
        precision=lax.Precision.HIGHEST,
        preferred_element_type=jnp.float32,
    )
    counts = (frames - jnp.abs(lag_offsets)).astype(jnp.float32)
    score = sums / jnp.sqrt(counts * head_size)[None, :]
    partial_logits = jnp.sum(head_weight[:, None] * score, axis=0)
    sync_logits = partial_logits
    step = 1
    while step < lines:
        pairs = [(i, i ^ step) for i in range(lines)]
        sync_logits = sync_logits + lax.ppermute(sync_logits, "tensor", pairs)
        step *= 2
    return (mixed, sync_logits[None, :])


def solution(mesh):
    return jax.shard_map(
        shards,
        mesh=mesh,
        in_specs=(
            P(("dp", "expert", "tensor"), None),
            P(),
            P(("dp", "expert", "tensor"), None),
            P(("dp", "expert", "tensor"), None),
            P(("dp", "expert", "tensor"), None, None),
            P(("dp", "expert", "tensor"), None, None),
            P(("dp", "expert", "tensor"), None, None),
            P(("dp", "expert", "tensor"), None, None),
            P(None, None, "tensor"),
            P("tensor"),
            P(("dp", "expert"), None, None),
            P(),
        ),
        out_specs=(P(("dp", "expert", "tensor"), None), P(("dp", "expert"), None)),
        check_vma=False,
    )
```

```python
import jax
import jax.numpy as jnp
from jax import lax
from jax.sharding import PartitionSpec as P


def dequant(weights, scales):
    block = weights.shape[0] // scales.shape[0]
    full = jnp.repeat(jnp.repeat(scales, block, axis=0), block, axis=1)
    return (weights.astype(jnp.float32) * full).astype(jnp.bfloat16)


def shards(
    tokens,
    norm_gain,
    expert_ids,
    gate_weights,
    w_in,
    scale_in,
    w_out,
    scale_out,
    w_sync,
    head_weight,
    frame_rows,
    lag_offsets,
):
    rows, width = tokens.shape
    top = expert_ids.shape[1]
    lines = lax.axis_size("tensor")
    plane = lax.axis_size(("dp", "expert"))
    experts_all = plane * lines * w_in.shape[0]
    most = 2 * rows * top // experts_all
    cap = lines * most
    here = lax.axis_index("tensor")
    x_float = tokens.astype(jnp.float32)
    normed = (
        x_float * lax.rsqrt(jnp.mean(x_float * x_float, axis=-1, keepdims=True) + 1e-06) * norm_gain
    ).astype(jnp.bfloat16)

    flat_ids = expert_ids.reshape(-1)
    pair_count = rows * top
    onehot = (flat_ids[:, None] == jnp.arange(experts_all, dtype=jnp.int32)[None, :]).astype(
        jnp.bfloat16
    )
    pair_index = jnp.arange(pair_count, dtype=jnp.int32)
    earlier = (pair_index[None, :] < pair_index[:, None]).astype(jnp.bfloat16)
    before = jnp.dot(earlier, onehot, preferred_element_type=jnp.float32)
    slots = jnp.sum(before * onehot.astype(jnp.float32), axis=1).reshape(rows, top)
    gate = gate_weights.astype(jnp.float32)
    gate_top = lax.reduce_precision(gate, exponent_bits=8, mantissa_bits=7)
    routing = jnp.concatenate(
        [
            expert_ids.astype(jnp.bfloat16),
            slots.astype(jnp.bfloat16),
            gate_top.astype(jnp.bfloat16),
            (gate - gate_top).astype(jnp.bfloat16),
        ],
        axis=1,
    )
    half = width // 2
    extra = rows * 4 * top // half
    padded = rows + 16
    packed = jnp.concatenate(
        [
            normed[:, :half],
            routing.reshape(extra, half),
            jnp.zeros((padded - rows - extra, half), jnp.bfloat16),
        ],
        axis=0,
    )
    line_a = lax.all_gather(packed, "tensor", axis=0, tiled=False)
    line_b = lax.all_gather(normed[:, half:], "tensor", axis=0, tiled=False)
    line_routing = line_a[:, rows : rows + extra, :].reshape(lines, rows, 4 * top)
    ids_l = line_routing[:, :, :top].astype(jnp.int32)
    slot_l = line_routing[:, :, top : 2 * top].astype(jnp.int32)
    gate_hi = line_routing[:, :, 2 * top : 3 * top].astype(jnp.float32)
    gate_lo = line_routing[:, :, 3 * top :].astype(jnp.float32)
    mine = (ids_l % lines) == here
    target = jnp.where(mine, (ids_l // lines) * most + slot_l, -1)
    slot_ids = jnp.arange(plane * most, dtype=jnp.int32)
    match = target[:, None, :, :] == slot_ids[None, :, None, None]
    select = jnp.any(match, axis=3)
    weight_hi = jnp.sum(jnp.where(match, gate_hi[:, None, :, :], 0.0), axis=3)
    weight_lo = jnp.sum(jnp.where(match, gate_lo[:, None, :, :], 0.0), axis=3)
    select = select.astype(jnp.bfloat16).reshape(lines, plane, most, rows)
    select_pad = jnp.pad(select, ((0, 0), (0, 0), (0, 0), (0, padded - rows)))
    weight_hi = weight_hi.astype(jnp.bfloat16).reshape(lines, plane, most, rows)
    weight_lo = weight_lo.astype(jnp.bfloat16).reshape(lines, plane, most, rows)
    line_parts = [line_a, line_b]
    select_parts = [select_pad, select]
    gate_up = dequant(w_in[0], scale_in[0])
    down_proj = dequant(w_out[0], scale_out[0])
    hidden_width = down_proj.shape[0]
    group = ("dp", "expert")

    def send(part):
        moved = lax.all_to_all(
            part.reshape(plane, cap, part.shape[1]), group, split_axis=0, concat_axis=0, tiled=True
        )
        return moved.reshape(plane * cap, part.shape[1])

    blocks = [
        send(
            jnp.einsum(
                "bpsr,brd->pbsd", select_parts[h], line_parts[h], preferred_element_type=jnp.float32
            )
            .astype(jnp.bfloat16)
            .reshape(plane * cap, half)
        )
        for h in range(2)
    ]
    mixed_in = jnp.dot(blocks[0], gate_up[:half], preferred_element_type=jnp.float32) + jnp.dot(
        blocks[1], gate_up[half:], preferred_element_type=jnp.float32
    )
    hidden = (jax.nn.silu(mixed_in[:, :hidden_width]) * mixed_in[:, hidden_width:]).astype(
        jnp.bfloat16
    )
    mixed_parts = []
    for h in range(2):
        output = jnp.dot(
            hidden, down_proj[:, h * half : (h + 1) * half], preferred_element_type=jnp.float32
        ).astype(jnp.bfloat16)
        back = send(output)
        back = back.reshape(plane, lines, most, half)
        partial = jnp.einsum(
            "bpsr,pbsd->brd", weight_hi, back, preferred_element_type=jnp.float32
        ) + jnp.einsum("bpsr,pbsd->brd", weight_lo, back, preferred_element_type=jnp.float32)
        combined = lax.psum_scatter(
            partial.reshape(lines * rows, half), "tensor", scatter_dimension=0, tiled=True
        )
        mixed_parts.append((x_float[:, h * half : (h + 1) * half] + combined).astype(jnp.bfloat16))
    mixed = jnp.concatenate(mixed_parts, axis=1)
    line_mixed = [
        lax.all_to_all(
            jnp.broadcast_to(mixed_parts[0][None], (lines, rows, half)),
            "tensor",
            split_axis=0,
            concat_axis=0,
            tiled=True,
        ).reshape(lines * rows, half),
        lax.all_gather(mixed_parts[1], "tensor", axis=0, tiled=True),
    ]

    local_sync = w_sync.reshape(width, -1)
    proj = (
        jnp.dot(line_mixed[0], local_sync[:half], preferred_element_type=jnp.float32)
        + jnp.dot(line_mixed[1], local_sync[half:], preferred_element_type=jnp.float32)
    ).astype(jnp.bfloat16)
    half = proj.shape[1] // 2
    heads_here = head_weight.shape[0]
    head_size = half // heads_here
    frames = frame_rows.shape[2]
    clip_len = proj.shape[0]
    clip_index = jnp.arange(clip_len, dtype=jnp.int32)
    pick_audio = (frame_rows[0, 0][:, None] == clip_index[None, :]).astype(jnp.bfloat16)
    pick_video = (frame_rows[0, 1][:, None] == clip_index[None, :]).astype(jnp.bfloat16)
    audio = (
        jnp.dot(pick_audio, proj[:, :half], preferred_element_type=jnp.float32)
        .astype(jnp.bfloat16)
        .reshape(frames, heads_here, head_size)
    )
    video = (
        jnp.dot(pick_video, proj[:, half:], preferred_element_type=jnp.float32)
        .astype(jnp.bfloat16)
        .reshape(frames, heads_here, head_size)
    )
    grams = jnp.einsum("thd,shd->hts", audio, video, preferred_element_type=jnp.float32)
    times = jnp.arange(frames, dtype=jnp.int32)
    offsets = times[None, :] - times[:, None]
    diagonal = (
        (offsets[None, :, :] == lag_offsets[:, None, None])
        .astype(jnp.float32)
        .reshape(lag_offsets.shape[0], frames * frames)
    )
    sums = lax.dot_general(
        grams.reshape(heads_here, frames * frames),
        diagonal,
        (((1,), (1,)), ((), ())),
        precision=lax.Precision.HIGHEST,
        preferred_element_type=jnp.float32,
    )
    counts = (frames - jnp.abs(lag_offsets)).astype(jnp.float32)
    score = sums / jnp.sqrt(counts * head_size)[None, :]
    partial_logits = jnp.sum(head_weight[:, None] * score, axis=0)
    sync_logits = partial_logits
    step = 1
    while step < lines:
        pairs = [(i, i ^ step) for i in range(lines)]
        sync_logits = sync_logits + lax.ppermute(sync_logits, "tensor", pairs)
        step *= 2
    return (mixed, sync_logits[None, :])


def solution(mesh):
    return jax.shard_map(
        shards,
        mesh=mesh,
        in_specs=(
            P(("dp", "expert", "tensor"), None),
            P(),
            P(("dp", "expert", "tensor"), None),
            P(("dp", "expert", "tensor"), None),
            P(("dp", "expert", "tensor"), None, None),
            P(("dp", "expert", "tensor"), None, None),
            P(("dp", "expert", "tensor"), None, None),
            P(("dp", "expert", "tensor"), None, None),
            P(None, None, "tensor"),
            P("tensor"),
            P(("dp", "expert"), None, None),
            P(),
        ),
        out_specs=(P(("dp", "expert", "tensor"), None), P(("dp", "expert"), None)),
        check_vma=False,
    )
```

```python
import jax
import jax.numpy as jnp
from jax import lax
from jax.sharding import PartitionSpec as P


def dequant(weights, scales):
    block = weights.shape[0] // scales.shape[0]
    full = jnp.repeat(jnp.repeat(scales, block, axis=0), block, axis=1)
    return (weights.astype(jnp.float32) * full).astype(jnp.bfloat16)


def shards(
    tokens,
    norm_gain,
    expert_ids,
    gate_weights,
    w_in,
    scale_in,
    w_out,
    scale_out,
    w_sync,
    head_weight,
    frame_rows,
    lag_offsets,
):
    rows, width = tokens.shape
    top = expert_ids.shape[1]
    lines = lax.axis_size("tensor")
    plane = lax.axis_size(("dp", "expert"))
    experts_all = plane * lines * w_in.shape[0]
    most = 2 * rows * top // experts_all
    cap = lines * most
    here = lax.axis_index("tensor")
    x_float = tokens.astype(jnp.float32)
    normed = (
        x_float * lax.rsqrt(jnp.mean(x_float * x_float, axis=-1, keepdims=True) + 1e-06) * norm_gain
    ).astype(jnp.bfloat16)

    flat_ids = expert_ids.reshape(-1)
    pair_count = rows * top
    onehot = (flat_ids[:, None] == jnp.arange(experts_all, dtype=jnp.int32)[None, :]).astype(
        jnp.bfloat16
    )
    pair_index = jnp.arange(pair_count, dtype=jnp.int32)
    earlier = (pair_index[None, :] < pair_index[:, None]).astype(jnp.bfloat16)
    before = jnp.dot(earlier, onehot, preferred_element_type=jnp.float32)
    slots = jnp.sum(before * onehot.astype(jnp.float32), axis=1).reshape(rows, top)
    gate = gate_weights.astype(jnp.float32)
    gate_top = lax.reduce_precision(gate, exponent_bits=8, mantissa_bits=7)
    routing = jnp.concatenate(
        [
            expert_ids.astype(jnp.bfloat16),
            slots.astype(jnp.bfloat16),
            gate_top.astype(jnp.bfloat16),
            (gate - gate_top).astype(jnp.bfloat16),
        ],
        axis=1,
    )
    half = width // 2
    extra = rows * 4 * top // half
    padded = rows + 16
    packed = jnp.concatenate(
        [
            normed[:, :half],
            routing.reshape(extra, half),
            jnp.zeros((padded - rows - extra, half), jnp.bfloat16),
        ],
        axis=0,
    )
    line_a = lax.all_gather(packed, "tensor", axis=0, tiled=False)
    line_b = lax.all_gather(normed[:, half:], "tensor", axis=0, tiled=False)
    line_routing = line_a[:, rows : rows + extra, :].reshape(lines, rows, 4 * top)
    ids_l = line_routing[:, :, :top].astype(jnp.int32)
    slot_l = line_routing[:, :, top : 2 * top].astype(jnp.int32)
    gate_hi = line_routing[:, :, 2 * top : 3 * top].astype(jnp.float32)
    gate_lo = line_routing[:, :, 3 * top :].astype(jnp.float32)
    mine = (ids_l % lines) == here
    target = jnp.where(mine, (ids_l // lines) * most + slot_l, -1)
    slot_ids = jnp.arange(plane * most, dtype=jnp.int32)
    match = target[:, None, :, :] == slot_ids[None, :, None, None]
    order = (here + jnp.arange(lines, dtype=jnp.int32)) % lines
    select = jnp.any(match, axis=3).astype(jnp.bfloat16).reshape(lines, plane, most, rows)
    select_rel = jnp.take(select, order[1:], axis=0)
    weight_hi = jnp.sum(jnp.where(match, gate_hi[:, None, :, :], 0.0), axis=3)
    weight_lo = jnp.sum(jnp.where(match, gate_lo[:, None, :, :], 0.0), axis=3)
    weight_hi = jnp.take(
        weight_hi.astype(jnp.bfloat16).reshape(lines, plane, most, rows), order, axis=0
    )
    weight_lo = jnp.take(
        weight_lo.astype(jnp.bfloat16).reshape(lines, plane, most, rows), order, axis=0
    )
    line_parts = [
        jnp.take(line_a[:, :rows], order[1:], axis=0),
        jnp.take(line_b, order[1:], axis=0),
    ]
    own_target = jnp.where(
        (expert_ids % lines) == here,
        (expert_ids // lines) * most + slots.astype(jnp.int32),
        -1,
    )
    own_select = jnp.any(
        own_target[None, :, :] == slot_ids[:, None, None], axis=2
    ).astype(jnp.bfloat16)
    gate_up = dequant(w_in[0], scale_in[0])
    down_proj = dequant(w_out[0], scale_out[0])
    hidden_width = down_proj.shape[0]
    group = ("dp", "expert")

    def send(part, depth):
        moved = lax.all_to_all(
            part.reshape(plane, depth, part.shape[-1]), group, split_axis=0, concat_axis=0, tiled=True
        )
        return moved.reshape(plane * depth, part.shape[-1])

    own_block = send(
        jnp.dot(own_select, normed, preferred_element_type=jnp.float32).astype(jnp.bfloat16), most
    )
    blocks = [
        send(
            jnp.einsum(
                "dpsr,drD->pdsD", select_rel, line_parts[h], preferred_element_type=jnp.float32
            ).astype(jnp.bfloat16),
            cap - most,
        )
        for h in range(2)
    ]
    own_in = jnp.dot(own_block, gate_up, preferred_element_type=jnp.float32)
    mixed_in = jnp.dot(blocks[0], gate_up[:half], preferred_element_type=jnp.float32) + jnp.dot(
        blocks[1], gate_up[half:], preferred_element_type=jnp.float32
    )
    mixed_in = jnp.concatenate(
        [
            own_in.reshape(plane, most, -1),
            mixed_in.reshape(plane, cap - most, -1),
        ],
        axis=1,
    ).reshape(plane * cap, -1)
    hidden = (jax.nn.silu(mixed_in[:, :hidden_width]) * mixed_in[:, hidden_width:]).astype(
        jnp.bfloat16
    )
    mixed_parts = []
    for h in range(2):
        output = jnp.dot(
            hidden, down_proj[:, h * half : (h + 1) * half], preferred_element_type=jnp.float32
        ).astype(jnp.bfloat16)
        back = send(output, cap)
        back = back.reshape(plane, lines, most, half)
        partial = jnp.einsum(
            "bpsr,pbsd->brd", weight_hi, back, preferred_element_type=jnp.float32
        ) + jnp.einsum("bpsr,pbsd->brd", weight_lo, back, preferred_element_type=jnp.float32)
        partial = jnp.take(partial, (jnp.arange(lines, dtype=jnp.int32) - here) % lines, axis=0)
        combined = lax.psum_scatter(
            partial.reshape(lines * rows, half), "tensor", scatter_dimension=0, tiled=True
        )
        mixed_parts.append(x_float[:, h * half : (h + 1) * half] + combined)
    mixed = jnp.concatenate(mixed_parts, axis=1).astype(jnp.bfloat16)

    local_sync = w_sync.reshape(width, -1)
    proj = jnp.dot(
        lax.all_gather(mixed, "tensor", axis=0, tiled=True),
        local_sync,
        preferred_element_type=jnp.float32,
    ).astype(jnp.bfloat16)
    half = proj.shape[1] // 2
    heads_here = head_weight.shape[0]
    head_size = half // heads_here
    frames = frame_rows.shape[2]
    clip_len = proj.shape[0]
    clip_index = jnp.arange(clip_len, dtype=jnp.int32)
    pick_audio = (frame_rows[0, 0][:, None] == clip_index[None, :]).astype(jnp.bfloat16)
    pick_video = (frame_rows[0, 1][:, None] == clip_index[None, :]).astype(jnp.bfloat16)
    audio = (
        jnp.dot(pick_audio, proj[:, :half], preferred_element_type=jnp.float32)
        .astype(jnp.bfloat16)
        .reshape(frames, heads_here, head_size)
    )
    video = (
        jnp.dot(pick_video, proj[:, half:], preferred_element_type=jnp.float32)
        .astype(jnp.bfloat16)
        .reshape(frames, heads_here, head_size)
    )
    grams = jnp.einsum("thd,shd->hts", audio, video, preferred_element_type=jnp.float32)
    times = jnp.arange(frames, dtype=jnp.int32)
    offsets = times[None, :] - times[:, None]
    diagonal = (
        (offsets[None, :, :] == lag_offsets[:, None, None])
        .astype(jnp.float32)
        .reshape(lag_offsets.shape[0], frames * frames)
    )
    sums = lax.dot_general(
        grams.reshape(heads_here, frames * frames),
        diagonal,
        (((1,), (1,)), ((), ())),
        precision=lax.Precision.HIGHEST,
        preferred_element_type=jnp.float32,
    )
    counts = (frames - jnp.abs(lag_offsets)).astype(jnp.float32)
    score = sums / jnp.sqrt(counts * head_size)[None, :]
    partial_logits = jnp.sum(head_weight[:, None] * score, axis=0)
    sync_logits = partial_logits
    step = 1
    while step < lines:
        pairs = [(i, i ^ step) for i in range(lines)]
        sync_logits = sync_logits + lax.ppermute(sync_logits, "tensor", pairs)
        step *= 2
    return (mixed, sync_logits[None, :])


def solution(mesh):
    return jax.shard_map(
        shards,
        mesh=mesh,
        in_specs=(
            P(("dp", "expert", "tensor"), None),
            P(),
            P(("dp", "expert", "tensor"), None),
            P(("dp", "expert", "tensor"), None),
            P(("dp", "expert", "tensor"), None, None),
            P(("dp", "expert", "tensor"), None, None),
            P(("dp", "expert", "tensor"), None, None),
            P(("dp", "expert", "tensor"), None, None),
            P(None, None, "tensor"),
            P("tensor"),
            P(("dp", "expert"), None, None),
            P(),
        ),
        out_specs=(P(("dp", "expert", "tensor"), None), P(("dp", "expert"), None)),
        check_vma=False,
    )
```

```python
import jax
import jax.numpy as jnp
from jax import lax
from jax.sharding import PartitionSpec as P


def dequant(weights, scales):
    block = weights.shape[0] // scales.shape[0]
    full = jnp.repeat(jnp.repeat(scales, block, axis=0), block, axis=1)
    return (weights.astype(jnp.float32) * full).astype(jnp.bfloat16)


def shards(
    tokens,
    norm_gain,
    expert_ids,
    gate_weights,
    w_in,
    scale_in,
    w_out,
    scale_out,
    w_sync,
    head_weight,
    frame_rows,
    lag_offsets,
):
    rows, width = tokens.shape
    top = expert_ids.shape[1]
    lines = lax.axis_size("tensor")
    plane = lax.axis_size(("dp", "expert"))
    experts_all = plane * lines * w_in.shape[0]
    most = 2 * rows * top // experts_all
    cap = lines * most
    here = lax.axis_index("tensor")
    x_float = tokens.astype(jnp.float32)
    normed = (
        x_float * lax.rsqrt(jnp.mean(x_float * x_float, axis=-1, keepdims=True) + 1e-06) * norm_gain
    ).astype(jnp.bfloat16)

    flat_ids = expert_ids.reshape(-1)
    pair_count = rows * top
    onehot = (flat_ids[:, None] == jnp.arange(experts_all, dtype=jnp.int32)[None, :]).astype(
        jnp.bfloat16
    )
    pair_index = jnp.arange(pair_count, dtype=jnp.int32)
    earlier = (pair_index[None, :] < pair_index[:, None]).astype(jnp.bfloat16)
    before = jnp.dot(earlier, onehot, preferred_element_type=jnp.float32)
    slots = jnp.sum(before * onehot.astype(jnp.float32), axis=1).reshape(rows, top)
    gate = gate_weights.astype(jnp.float32)
    gate_top = lax.reduce_precision(gate, exponent_bits=8, mantissa_bits=7)
    routing = jnp.concatenate(
        [
            expert_ids.astype(jnp.bfloat16),
            slots.astype(jnp.bfloat16),
            gate_top.astype(jnp.bfloat16),
            (gate - gate_top).astype(jnp.bfloat16),
        ],
        axis=1,
    )
    half = width // 2
    extra = rows * 4 * top // half
    padded = rows + 16
    packed = jnp.concatenate(
        [
            normed[:, :half],
            routing.reshape(extra, half),
            jnp.zeros((padded - rows - extra, half), jnp.bfloat16),
        ],
        axis=0,
    )
    line_a = lax.all_gather(packed, "tensor", axis=0, tiled=False)
    line_b = lax.all_gather(normed[:, half:], "tensor", axis=0, tiled=False)
    line_routing = line_a[:, rows : rows + extra, :].reshape(lines, rows, 4 * top)
    ids_l = line_routing[:, :, :top].astype(jnp.int32)
    slot_l = line_routing[:, :, top : 2 * top].astype(jnp.int32)
    gate_hi = line_routing[:, :, 2 * top : 3 * top].astype(jnp.float32)
    gate_lo = line_routing[:, :, 3 * top :].astype(jnp.float32)
    mine = (ids_l % lines) == here
    target = jnp.where(mine, (ids_l // lines) * most + slot_l, -1)
    slot_ids = jnp.arange(plane * most, dtype=jnp.int32)
    match = target[:, None, :, :] == slot_ids[None, :, None, None]
    order = (here + jnp.arange(lines, dtype=jnp.int32)) % lines
    select = jnp.any(match, axis=3).astype(jnp.bfloat16).reshape(lines, plane, most, rows)
    select_rel = jnp.take(select, order[1:], axis=0)
    weight_hi = jnp.sum(jnp.where(match, gate_hi[:, None, :, :], 0.0), axis=3)
    weight_lo = jnp.sum(jnp.where(match, gate_lo[:, None, :, :], 0.0), axis=3)
    weight_hi = jnp.take(
        weight_hi.astype(jnp.bfloat16).reshape(lines, plane, most, rows), order, axis=0
    )
    weight_lo = jnp.take(
        weight_lo.astype(jnp.bfloat16).reshape(lines, plane, most, rows), order, axis=0
    )
    line_parts = [
        jnp.take(line_a[:, :rows], order[1:], axis=0),
        jnp.take(line_b, order[1:], axis=0),
    ]
    own_target = jnp.where(
        (expert_ids % lines) == here,
        (expert_ids // lines) * most + slots.astype(jnp.int32),
        -1,
    )
    own_select = jnp.any(
        own_target[None, :, :] == slot_ids[:, None, None], axis=2
    ).astype(jnp.bfloat16)
    gate_up = dequant(w_in[0], scale_in[0])
    down_proj = dequant(w_out[0], scale_out[0])
    hidden_width = down_proj.shape[0]
    group = ("dp", "expert")

    def send(part, depth):
        moved = lax.all_to_all(
            part.reshape(plane, depth, part.shape[-1]), group, split_axis=0, concat_axis=0, tiled=True
        )
        return moved.reshape(plane * depth, part.shape[-1])

    own_block = send(
        jnp.dot(own_select, normed, preferred_element_type=jnp.float32).astype(jnp.bfloat16), most
    )
    blocks = [
        send(
            jnp.einsum(
                "dpsr,drD->pdsD", select_rel, line_parts[h], preferred_element_type=jnp.float32
            ).astype(jnp.bfloat16),
            cap - most,
        )
        for h in range(2)
    ]
    own_in = jnp.dot(own_block, gate_up, preferred_element_type=jnp.float32)
    mixed_in = jnp.dot(blocks[0], gate_up[:half], preferred_element_type=jnp.float32) + jnp.dot(
        blocks[1], gate_up[half:], preferred_element_type=jnp.float32
    )
    mixed_in = jnp.concatenate(
        [
            own_in.reshape(plane, most, -1),
            mixed_in.reshape(plane, cap - most, -1),
        ],
        axis=1,
    ).reshape(plane * cap, -1)
    hidden = (jax.nn.silu(mixed_in[:, :hidden_width]) * mixed_in[:, hidden_width:]).astype(
        jnp.bfloat16
    )
    mixed_parts = []
    scattered = None
    for h in range(2):
        output = jnp.dot(
            hidden, down_proj[:, h * half : (h + 1) * half], preferred_element_type=jnp.float32
        ).astype(jnp.bfloat16)
        if scattered is not None:
            scattered, output = lax.optimization_barrier((scattered, output))
        back = send(output, cap)
        back = back.reshape(plane, lines, most, half)
        partial = jnp.einsum(
            "bpsr,pbsd->brd", weight_hi, back, preferred_element_type=jnp.float32
        ) + jnp.einsum("bpsr,pbsd->brd", weight_lo, back, preferred_element_type=jnp.float32)
        partial = jnp.take(partial, (jnp.arange(lines, dtype=jnp.int32) - here) % lines, axis=0)
        scattered = partial.reshape(lines * rows, half)
        mixed_parts.append(scattered)
    for h in range(2):
        combined = lax.psum_scatter(mixed_parts[h], "tensor", scatter_dimension=0, tiled=True)
        mixed_parts[h] = x_float[:, h * half : (h + 1) * half] + combined
    mixed = jnp.concatenate(mixed_parts, axis=1).astype(jnp.bfloat16)

    local_sync = w_sync.reshape(width, -1)
    proj = jnp.dot(
        lax.all_gather(mixed, "tensor", axis=0, tiled=True),
        local_sync,
        preferred_element_type=jnp.float32,
    ).astype(jnp.bfloat16)
    half = proj.shape[1] // 2
    heads_here = head_weight.shape[0]
    head_size = half // heads_here
    frames = frame_rows.shape[2]
    clip_len = proj.shape[0]
    clip_index = jnp.arange(clip_len, dtype=jnp.int32)
    pick_audio = (frame_rows[0, 0][:, None] == clip_index[None, :]).astype(jnp.bfloat16)
    pick_video = (frame_rows[0, 1][:, None] == clip_index[None, :]).astype(jnp.bfloat16)
    audio = (
        jnp.dot(pick_audio, proj[:, :half], preferred_element_type=jnp.float32)
        .astype(jnp.bfloat16)
        .reshape(frames, heads_here, head_size)
    )
    video = (
        jnp.dot(pick_video, proj[:, half:], preferred_element_type=jnp.float32)
        .astype(jnp.bfloat16)
        .reshape(frames, heads_here, head_size)
    )
    grams = jnp.einsum("thd,shd->hts", audio, video, preferred_element_type=jnp.float32)
    times = jnp.arange(frames, dtype=jnp.int32)
    offsets = times[None, :] - times[:, None]
    diagonal = (
        (offsets[None, :, :] == lag_offsets[:, None, None])
        .astype(jnp.float32)
        .reshape(lag_offsets.shape[0], frames * frames)
    )
    sums = lax.dot_general(
        grams.reshape(heads_here, frames * frames),
        diagonal,
        (((1,), (1,)), ((), ())),
        precision=lax.Precision.HIGHEST,
        preferred_element_type=jnp.float32,
    )
    counts = (frames - jnp.abs(lag_offsets)).astype(jnp.float32)
    score = sums / jnp.sqrt(counts * head_size)[None, :]
    partial_logits = jnp.sum(head_weight[:, None] * score, axis=0)
    sync_logits = partial_logits
    step = 1
    while step < lines:
        pairs = [(i, i ^ step) for i in range(lines)]
        sync_logits = sync_logits + lax.ppermute(sync_logits, "tensor", pairs)
        step *= 2
    return (mixed, sync_logits[None, :])


def solution(mesh):
    return jax.shard_map(
        shards,
        mesh=mesh,
        in_specs=(
            P(("dp", "expert", "tensor"), None),
            P(),
            P(("dp", "expert", "tensor"), None),
            P(("dp", "expert", "tensor"), None),
            P(("dp", "expert", "tensor"), None, None),
            P(("dp", "expert", "tensor"), None, None),
            P(("dp", "expert", "tensor"), None, None),
            P(("dp", "expert", "tensor"), None, None),
            P(None, None, "tensor"),
            P("tensor"),
            P(("dp", "expert"), None, None),
            P(),
        ),
        out_specs=(P(("dp", "expert", "tensor"), None), P(("dp", "expert"), None)),
        check_vma=False,
    )
```

```python
import jax
import jax.numpy as jnp
from jax import lax
from jax.sharding import PartitionSpec as P


def dequant(weights, scales):
    block = weights.shape[0] // scales.shape[0]
    full = jnp.repeat(jnp.repeat(scales, block, axis=0), block, axis=1)
    return (weights.astype(jnp.float32) * full).astype(jnp.bfloat16)


def shards(
    tokens,
    norm_gain,
    expert_ids,
    gate_weights,
    w_in,
    scale_in,
    w_out,
    scale_out,
    w_sync,
    head_weight,
    frame_rows,
    lag_offsets,
):
    rows, width = tokens.shape
    top = expert_ids.shape[1]
    lines = lax.axis_size("tensor")
    plane = lax.axis_size(("dp", "expert"))
    experts_all = plane * lines * w_in.shape[0]
    most = 2 * rows * top // experts_all
    cap = lines * most
    here = lax.axis_index("tensor")
    x_float = tokens.astype(jnp.float32)
    normed = (
        x_float * lax.rsqrt(jnp.mean(x_float * x_float, axis=-1, keepdims=True) + 1e-06) * norm_gain
    ).astype(jnp.bfloat16)

    flat_ids = expert_ids.reshape(-1)
    pair_count = rows * top
    onehot = (flat_ids[:, None] == jnp.arange(experts_all, dtype=jnp.int32)[None, :]).astype(
        jnp.bfloat16
    )
    pair_index = jnp.arange(pair_count, dtype=jnp.int32)
    earlier = (pair_index[None, :] < pair_index[:, None]).astype(jnp.bfloat16)
    before = jnp.dot(earlier, onehot, preferred_element_type=jnp.float32)
    slots = jnp.sum(before * onehot.astype(jnp.float32), axis=1).reshape(rows, top)
    gate = gate_weights.astype(jnp.float32)
    gate_top = lax.reduce_precision(gate, exponent_bits=8, mantissa_bits=7)
    routing = jnp.concatenate(
        [
            expert_ids.astype(jnp.bfloat16),
            slots.astype(jnp.bfloat16),
            gate_top.astype(jnp.bfloat16),
            (gate - gate_top).astype(jnp.bfloat16),
        ],
        axis=1,
    )
    half = width // 2
    extra = rows * 4 * top // half
    padded = rows + 16
    packed = jnp.concatenate(
        [
            normed[:, :half],
            routing.reshape(extra, half),
            jnp.zeros((padded - rows - extra, half), jnp.bfloat16),
        ],
        axis=0,
    )
    line_a = lax.all_gather(packed, "tensor", axis=0, tiled=False)
    line_b = lax.all_gather(normed[:, half:], "tensor", axis=0, tiled=False)
    line_routing = line_a[:, rows : rows + extra, :].reshape(lines, rows, 4 * top)
    ids_l = line_routing[:, :, :top].astype(jnp.int32)
    slot_l = line_routing[:, :, top : 2 * top].astype(jnp.int32)
    gate_hi = line_routing[:, :, 2 * top : 3 * top].astype(jnp.float32)
    gate_lo = line_routing[:, :, 3 * top :].astype(jnp.float32)
    mine = (ids_l % lines) == here
    target = jnp.where(mine, (ids_l // lines) * most + slot_l, -1)
    slot_ids = jnp.arange(plane * most, dtype=jnp.int32)
    match = target[:, None, :, :] == slot_ids[None, :, None, None]
    order = (here + jnp.arange(lines, dtype=jnp.int32)) % lines
    select = jnp.any(match, axis=3).astype(jnp.bfloat16).reshape(lines, plane, most, rows)
    select_rel = jnp.take(select, order[1:], axis=0)
    weight_hi = jnp.sum(jnp.where(match, gate_hi[:, None, :, :], 0.0), axis=3)
    weight_lo = jnp.sum(jnp.where(match, gate_lo[:, None, :, :], 0.0), axis=3)
    weight_hi = jnp.take(
        weight_hi.astype(jnp.bfloat16).reshape(lines, plane, most, rows), order, axis=0
    )
    weight_lo = jnp.take(
        weight_lo.astype(jnp.bfloat16).reshape(lines, plane, most, rows), order, axis=0
    )
    line_parts = [
        jnp.take(line_a[:, :rows], order[1:], axis=0),
        jnp.take(line_b, order[1:], axis=0),
    ]
    own_target = jnp.where(
        (expert_ids % lines) == here,
        (expert_ids // lines) * most + slots.astype(jnp.int32),
        -1,
    )
    own_select = jnp.any(
        own_target[None, :, :] == slot_ids[:, None, None], axis=2
    ).astype(jnp.bfloat16)
    gate_up = dequant(w_in[0], scale_in[0])
    down_proj = dequant(w_out[0], scale_out[0])
    hidden_width = down_proj.shape[0]
    group = ("dp", "expert")

    def send(part, depth):
        moved = lax.all_to_all(
            part.reshape(plane, depth, part.shape[-1]), group, split_axis=0, concat_axis=0, tiled=True
        )
        return moved.reshape(plane * depth, part.shape[-1])

    own_block = send(
        jnp.dot(own_select, normed, preferred_element_type=jnp.float32).astype(jnp.bfloat16), most
    )
    blocks = [
        send(
            jnp.einsum(
                "dpsr,drD->pdsD", select_rel, line_parts[h], preferred_element_type=jnp.float32
            ).astype(jnp.bfloat16),
            cap - most,
        )
        for h in range(2)
    ]
    def activate(mixed_in):
        return (jax.nn.silu(mixed_in[:, :hidden_width]) * mixed_in[:, hidden_width:]).astype(
            jnp.bfloat16
        )

    own_hidden = activate(jnp.dot(own_block, gate_up, preferred_element_type=jnp.float32))
    rest_hidden = activate(
        jnp.dot(blocks[0], gate_up[:half], preferred_element_type=jnp.float32)
        + jnp.dot(blocks[1], gate_up[half:], preferred_element_type=jnp.float32)
    )
    hidden = jnp.concatenate(
        [
            own_hidden.reshape(plane, most, hidden_width),
            rest_hidden.reshape(plane, cap - most, hidden_width),
        ],
        axis=1,
    ).reshape(plane * cap, hidden_width)
    mixed_parts = []
    scattered = None
    for h in range(2):
        output = jnp.dot(
            hidden, down_proj[:, h * half : (h + 1) * half], preferred_element_type=jnp.float32
        ).astype(jnp.bfloat16)
        if scattered is not None:
            scattered, output = lax.optimization_barrier((scattered, output))
        back = send(output, cap)
        back = back.reshape(plane, lines, most, half)
        partial = jnp.einsum(
            "bpsr,pbsd->brd", weight_hi, back, preferred_element_type=jnp.float32
        ) + jnp.einsum("bpsr,pbsd->brd", weight_lo, back, preferred_element_type=jnp.float32)
        partial = jnp.take(partial, (jnp.arange(lines, dtype=jnp.int32) - here) % lines, axis=0)
        scattered = partial.reshape(lines * rows, half)
        mixed_parts.append(scattered)
    for h in range(2):
        combined = lax.psum_scatter(mixed_parts[h], "tensor", scatter_dimension=0, tiled=True)
        mixed_parts[h] = x_float[:, h * half : (h + 1) * half] + combined
    mixed = jnp.concatenate(mixed_parts, axis=1).astype(jnp.bfloat16)

    local_sync = w_sync.reshape(width, -1)
    proj = jnp.dot(
        lax.all_gather(mixed, "tensor", axis=0, tiled=True),
        local_sync,
        preferred_element_type=jnp.float32,
    ).astype(jnp.bfloat16)
    half = proj.shape[1] // 2
    heads_here = head_weight.shape[0]
    head_size = half // heads_here
    frames = frame_rows.shape[2]
    clip_len = proj.shape[0]
    clip_index = jnp.arange(clip_len, dtype=jnp.int32)
    pick_audio = (frame_rows[0, 0][:, None] == clip_index[None, :]).astype(jnp.bfloat16)
    pick_video = (frame_rows[0, 1][:, None] == clip_index[None, :]).astype(jnp.bfloat16)
    audio = (
        jnp.dot(pick_audio, proj[:, :half], preferred_element_type=jnp.float32)
        .astype(jnp.bfloat16)
        .reshape(frames, heads_here, head_size)
    )
    video = (
        jnp.dot(pick_video, proj[:, half:], preferred_element_type=jnp.float32)
        .astype(jnp.bfloat16)
        .reshape(frames, heads_here, head_size)
    )
    grams = jnp.einsum("thd,shd->hts", audio, video, preferred_element_type=jnp.float32)
    times = jnp.arange(frames, dtype=jnp.int32)
    offsets = times[None, :] - times[:, None]
    diagonal = (
        (offsets[None, :, :] == lag_offsets[:, None, None])
        .astype(jnp.float32)
        .reshape(lag_offsets.shape[0], frames * frames)
    )
    sums = lax.dot_general(
        grams.reshape(heads_here, frames * frames),
        diagonal,
        (((1,), (1,)), ((), ())),
        precision=lax.Precision.HIGHEST,
        preferred_element_type=jnp.float32,
    )
    counts = (frames - jnp.abs(lag_offsets)).astype(jnp.float32)
    score = sums / jnp.sqrt(counts * head_size)[None, :]
    partial_logits = jnp.sum(head_weight[:, None] * score, axis=0)
    sync_logits = partial_logits
    step = 1
    while step < lines:
        pairs = [(i, i ^ step) for i in range(lines)]
        sync_logits = sync_logits + lax.ppermute(sync_logits, "tensor", pairs)
        step *= 2
    return (mixed, sync_logits[None, :])


def solution(mesh):
    return jax.shard_map(
        shards,
        mesh=mesh,
        in_specs=(
            P(("dp", "expert", "tensor"), None),
            P(),
            P(("dp", "expert", "tensor"), None),
            P(("dp", "expert", "tensor"), None),
            P(("dp", "expert", "tensor"), None, None),
            P(("dp", "expert", "tensor"), None, None),
            P(("dp", "expert", "tensor"), None, None),
            P(("dp", "expert", "tensor"), None, None),
            P(None, None, "tensor"),
            P("tensor"),
            P(("dp", "expert"), None, None),
            P(),
        ),
        out_specs=(P(("dp", "expert", "tensor"), None), P(("dp", "expert"), None)),
        check_vma=False,
    )
```

```python
import jax
import jax.numpy as jnp
from jax import lax
from jax.sharding import PartitionSpec as P


def dequant(weights, scales):
    block = weights.shape[0] // scales.shape[0]
    full = jnp.repeat(jnp.repeat(scales, block, axis=0), block, axis=1)
    return (weights.astype(jnp.float32) * full).astype(jnp.bfloat16)


def shards(
    tokens,
    norm_gain,
    expert_ids,
    gate_weights,
    w_in,
    scale_in,
    w_out,
    scale_out,
    w_sync,
    head_weight,
    frame_rows,
    lag_offsets,
):
    rows, width = tokens.shape
    top = expert_ids.shape[1]
    lines = lax.axis_size("tensor")
    plane = lax.axis_size(("dp", "expert"))
    experts_all = plane * lines * w_in.shape[0]
    most = 2 * rows * top // experts_all
    cap = lines * most
    here = lax.axis_index("tensor")
    x_float = tokens.astype(jnp.float32)
    normed = (
        x_float * lax.rsqrt(jnp.mean(x_float * x_float, axis=-1, keepdims=True) + 1e-06) * norm_gain
    ).astype(jnp.bfloat16)

    flat_ids = expert_ids.reshape(-1)
    pair_count = rows * top
    onehot = (flat_ids[:, None] == jnp.arange(experts_all, dtype=jnp.int32)[None, :]).astype(
        jnp.bfloat16
    )
    pair_index = jnp.arange(pair_count, dtype=jnp.int32)
    earlier = (pair_index[None, :] < pair_index[:, None]).astype(jnp.bfloat16)
    before = jnp.dot(earlier, onehot, preferred_element_type=jnp.float32)
    slots = jnp.sum(before * onehot.astype(jnp.float32), axis=1).reshape(rows, top)
    gate = gate_weights.astype(jnp.float32)
    gate_top = lax.reduce_precision(gate, exponent_bits=8, mantissa_bits=7)
    routing = jnp.concatenate(
        [
            expert_ids.astype(jnp.bfloat16),
            slots.astype(jnp.bfloat16),
            gate_top.astype(jnp.bfloat16),
            (gate - gate_top).astype(jnp.bfloat16),
        ],
        axis=1,
    )
    half = width // 2
    extra = rows * 4 * top // half
    padded = rows + 16
    packed = jnp.concatenate(
        [
            normed[:, :half],
            routing.reshape(extra, half),
            jnp.zeros((padded - rows - extra, half), jnp.bfloat16),
        ],
        axis=0,
    )
    line_a = lax.all_gather(packed, "tensor", axis=0, tiled=False)
    line_b = lax.all_gather(normed[:, half:], "tensor", axis=0, tiled=False)
    line_routing = line_a[:, rows : rows + extra, :].reshape(lines, rows, 4 * top)
    ids_l = line_routing[:, :, :top].astype(jnp.int32)
    slot_l = line_routing[:, :, top : 2 * top].astype(jnp.int32)
    gate_hi = line_routing[:, :, 2 * top : 3 * top].astype(jnp.float32)
    gate_lo = line_routing[:, :, 3 * top :].astype(jnp.float32)
    mine = (ids_l % lines) == here
    target = jnp.where(mine, (ids_l // lines) * most + slot_l, -1)
    slot_ids = jnp.arange(plane * most, dtype=jnp.int32)
    match = target[:, None, :, :] == slot_ids[None, :, None, None]
    order = (here + jnp.arange(lines, dtype=jnp.int32)) % lines
    select = jnp.any(match, axis=3).astype(jnp.bfloat16).reshape(lines, plane, most, rows)
    select_rel = jnp.take(select, order[1:], axis=0)
    weight_hi = jnp.sum(jnp.where(match, gate_hi[:, None, :, :], 0.0), axis=3)
    weight_lo = jnp.sum(jnp.where(match, gate_lo[:, None, :, :], 0.0), axis=3)
    weight_hi = weight_hi.astype(jnp.bfloat16).reshape(lines, plane, most, rows)
    weight_lo = weight_lo.astype(jnp.bfloat16).reshape(lines, plane, most, rows)
    line_parts = [
        jnp.take(line_a[:, :rows], order[1:], axis=0),
        jnp.take(line_b, order[1:], axis=0),
    ]
    own_target = jnp.where(
        (expert_ids % lines) == here,
        (expert_ids // lines) * most + slots.astype(jnp.int32),
        -1,
    )
    own_select = jnp.any(
        own_target[None, :, :] == slot_ids[:, None, None], axis=2
    ).astype(jnp.bfloat16)
    gate_up = dequant(w_in[0], scale_in[0])
    down_proj = dequant(w_out[0], scale_out[0])
    hidden_width = down_proj.shape[0]
    group = ("dp", "expert")

    def send(part, depth):
        moved = lax.all_to_all(
            part.reshape(plane, depth, part.shape[-1]), group, split_axis=0, concat_axis=0, tiled=True
        )
        return moved.reshape(plane * depth, part.shape[-1])

    own_block = send(
        jnp.dot(own_select, normed, preferred_element_type=jnp.float32).astype(jnp.bfloat16), most
    )
    blocks = [
        send(
            jnp.einsum(
                "dpsr,drD->pdsD", select_rel, line_parts[h], preferred_element_type=jnp.float32
            ).astype(jnp.bfloat16),
            cap - most,
        )
        for h in range(2)
    ]
    def activate(mixed_in):
        return (jax.nn.silu(mixed_in[:, :hidden_width]) * mixed_in[:, hidden_width:]).astype(
            jnp.bfloat16
        )

    own_hidden = activate(jnp.dot(own_block, gate_up, preferred_element_type=jnp.float32))
    rest_hidden = activate(
        jnp.dot(blocks[0], gate_up[:half], preferred_element_type=jnp.float32)
        + jnp.dot(blocks[1], gate_up[half:], preferred_element_type=jnp.float32)
    )
    hidden = jnp.concatenate(
        [
            own_hidden.reshape(plane, 1, most, hidden_width),
            rest_hidden.reshape(plane, lines - 1, most, hidden_width),
        ],
        axis=1,
    )
    hidden = jnp.take(
        hidden, (jnp.arange(lines, dtype=jnp.int32) - here) % lines, axis=1
    ).reshape(plane * cap, hidden_width)
    mixed_parts = []
    scattered = None
    for h in range(2):
        output = jnp.dot(
            hidden, down_proj[:, h * half : (h + 1) * half], preferred_element_type=jnp.float32
        ).astype(jnp.bfloat16)
        if scattered is not None:
            scattered, output = lax.optimization_barrier((scattered, output))
        back = send(output, cap)
        back = back.reshape(plane, lines, most, half)
        partial = jnp.einsum(
            "bpsr,pbsd->brd", weight_hi, back, preferred_element_type=jnp.float32
        ) + jnp.einsum("bpsr,pbsd->brd", weight_lo, back, preferred_element_type=jnp.float32)
        scattered = partial.reshape(lines * rows, half)
        mixed_parts.append(scattered)
    for h in range(2):
        combined = lax.psum_scatter(mixed_parts[h], "tensor", scatter_dimension=0, tiled=True)
        mixed_parts[h] = x_float[:, h * half : (h + 1) * half] + combined
    mixed = jnp.concatenate(mixed_parts, axis=1).astype(jnp.bfloat16)

    local_sync = w_sync.reshape(width, -1)
    proj = jnp.dot(
        lax.all_gather(mixed, "tensor", axis=0, tiled=True),
        local_sync,
        preferred_element_type=jnp.float32,
    ).astype(jnp.bfloat16)
    half = proj.shape[1] // 2
    heads_here = head_weight.shape[0]
    head_size = half // heads_here
    frames = frame_rows.shape[2]
    clip_len = proj.shape[0]
    clip_index = jnp.arange(clip_len, dtype=jnp.int32)
    pick_audio = (frame_rows[0, 0][:, None] == clip_index[None, :]).astype(jnp.bfloat16)
    pick_video = (frame_rows[0, 1][:, None] == clip_index[None, :]).astype(jnp.bfloat16)
    audio = (
        jnp.dot(pick_audio, proj[:, :half], preferred_element_type=jnp.float32)
        .astype(jnp.bfloat16)
        .reshape(frames, heads_here, head_size)
    )
    video = (
        jnp.dot(pick_video, proj[:, half:], preferred_element_type=jnp.float32)
        .astype(jnp.bfloat16)
        .reshape(frames, heads_here, head_size)
    )
    grams = jnp.einsum("thd,shd->hts", audio, video, preferred_element_type=jnp.float32)
    times = jnp.arange(frames, dtype=jnp.int32)
    offsets = times[None, :] - times[:, None]
    diagonal = (
        (offsets[None, :, :] == lag_offsets[:, None, None])
        .astype(jnp.float32)
        .reshape(lag_offsets.shape[0], frames * frames)
    )
    sums = lax.dot_general(
        grams.reshape(heads_here, frames * frames),
        diagonal,
        (((1,), (1,)), ((), ())),
        precision=lax.Precision.HIGHEST,
        preferred_element_type=jnp.float32,
    )
    counts = (frames - jnp.abs(lag_offsets)).astype(jnp.float32)
    score = sums / jnp.sqrt(counts * head_size)[None, :]
    partial_logits = jnp.sum(head_weight[:, None] * score, axis=0)
    sync_logits = partial_logits
    step = 1
    while step < lines:
        pairs = [(i, i ^ step) for i in range(lines)]
        sync_logits = sync_logits + lax.ppermute(sync_logits, "tensor", pairs)
        step *= 2
    return (mixed, sync_logits[None, :])


def solution(mesh):
    return jax.shard_map(
        shards,
        mesh=mesh,
        in_specs=(
            P(("dp", "expert", "tensor"), None),
            P(),
            P(("dp", "expert", "tensor"), None),
            P(("dp", "expert", "tensor"), None),
            P(("dp", "expert", "tensor"), None, None),
            P(("dp", "expert", "tensor"), None, None),
            P(("dp", "expert", "tensor"), None, None),
            P(("dp", "expert", "tensor"), None, None),
            P(None, None, "tensor"),
            P("tensor"),
            P(("dp", "expert"), None, None),
            P(),
        ),
        out_specs=(P(("dp", "expert", "tensor"), None), P(("dp", "expert"), None)),
        check_vma=False,
    )
```

```python
import jax
import jax.numpy as jnp
from jax import lax
from jax.sharding import PartitionSpec as P


def dequant(weights, scales):
    block = weights.shape[0] // scales.shape[0]
    full = jnp.repeat(jnp.repeat(scales, block, axis=0), block, axis=1)
    return (weights.astype(jnp.float32) * full).astype(jnp.bfloat16)


def shards(
    tokens,
    norm_gain,
    expert_ids,
    gate_weights,
    w_in,
    scale_in,
    w_out,
    scale_out,
    w_sync,
    head_weight,
    frame_rows,
    lag_offsets,
):
    rows, width = tokens.shape
    top = expert_ids.shape[1]
    lines = lax.axis_size("tensor")
    plane = lax.axis_size(("dp", "expert"))
    experts_all = plane * lines * w_in.shape[0]
    most = 2 * rows * top // experts_all
    cap = lines * most
    here = lax.axis_index("tensor")
    x_float = tokens.astype(jnp.float32)
    normed = (
        x_float * lax.rsqrt(jnp.mean(x_float * x_float, axis=-1, keepdims=True) + 1e-06) * norm_gain
    ).astype(jnp.bfloat16)

    flat_ids = expert_ids.reshape(-1)
    pair_count = rows * top
    onehot = (flat_ids[:, None] == jnp.arange(experts_all, dtype=jnp.int32)[None, :]).astype(
        jnp.bfloat16
    )
    pair_index = jnp.arange(pair_count, dtype=jnp.int32)
    earlier = (pair_index[None, :] < pair_index[:, None]).astype(jnp.bfloat16)
    before = jnp.dot(earlier, onehot, preferred_element_type=jnp.float32)
    slots = jnp.sum(before * onehot.astype(jnp.float32), axis=1).reshape(rows, top)
    gate = gate_weights.astype(jnp.float32)
    gate_top = lax.reduce_precision(gate, exponent_bits=8, mantissa_bits=7)
    routing = jnp.concatenate(
        [
            expert_ids.astype(jnp.bfloat16),
            slots.astype(jnp.bfloat16),
            gate_top.astype(jnp.bfloat16),
            (gate - gate_top).astype(jnp.bfloat16),
        ],
        axis=1,
    )
    half = width // 2
    extra = rows * 4 * top // half
    padded = rows + 16
    packed = jnp.concatenate(
        [
            normed[:, :half],
            routing.reshape(extra, half),
            jnp.zeros((padded - rows - extra, half), jnp.bfloat16),
        ],
        axis=0,
    )
    line_a = lax.all_gather(packed, "tensor", axis=0, tiled=False)
    line_b = lax.all_gather(normed[:, half:], "tensor", axis=0, tiled=False)
    line_routing = line_a[:, rows : rows + extra, :].reshape(lines, rows, 4 * top)
    ids_l = line_routing[:, :, :top].astype(jnp.int32)
    slot_l = line_routing[:, :, top : 2 * top].astype(jnp.int32)
    gate_hi = line_routing[:, :, 2 * top : 3 * top].astype(jnp.float32)
    gate_lo = line_routing[:, :, 3 * top :].astype(jnp.float32)
    mine = (ids_l % lines) == here
    target = jnp.where(mine, (ids_l // lines) * most + slot_l, -1)
    slot_ids = jnp.arange(plane * most, dtype=jnp.int32)
    match = target[:, None, :, :] == slot_ids[None, :, None, None]
    order = (here + jnp.arange(lines, dtype=jnp.int32)) % lines
    select = jnp.any(match, axis=3).astype(jnp.bfloat16).reshape(lines, plane, most, rows)
    select_rel = jnp.take(select, order[1:], axis=0)
    weight_hi = jnp.sum(jnp.where(match, gate_hi[:, None, :, :], 0.0), axis=3)
    weight_lo = jnp.sum(jnp.where(match, gate_lo[:, None, :, :], 0.0), axis=3)
    weight_hi = weight_hi.astype(jnp.bfloat16).reshape(lines, plane, most, rows)
    weight_lo = weight_lo.astype(jnp.bfloat16).reshape(lines, plane, most, rows)
    line_parts = [
        jnp.take(line_a[:, :rows], order[1:], axis=0),
        jnp.take(line_b, order[1:], axis=0),
    ]
    own_target = jnp.where(
        (expert_ids % lines) == here,
        (expert_ids // lines) * most + slots.astype(jnp.int32),
        -1,
    )
    own_select = jnp.any(
        own_target[None, :, :] == slot_ids[:, None, None], axis=2
    ).astype(jnp.bfloat16)
    gate_up = dequant(w_in[0], scale_in[0])
    down_proj = dequant(w_out[0], scale_out[0])
    hidden_width = down_proj.shape[0]
    group = ("dp", "expert")

    def send(part, depth):
        moved = lax.all_to_all(
            part.reshape(plane, depth, part.shape[-1]), group, split_axis=0, concat_axis=0, tiled=True
        )
        return moved.reshape(plane * depth, part.shape[-1])

    own_block = send(
        jnp.dot(own_select, normed, preferred_element_type=jnp.float32).astype(jnp.bfloat16), most
    )
    blocks = [
        send(
            jnp.einsum(
                "dpsr,drD->pdsD", select_rel, line_parts[h], preferred_element_type=jnp.float32
            ).astype(jnp.bfloat16),
            cap - most,
        )
        for h in range(2)
    ]
    def activate(mixed_in):
        return (jax.nn.silu(mixed_in[:, :hidden_width]) * mixed_in[:, hidden_width:]).astype(
            jnp.bfloat16
        )

    own_hidden = activate(jnp.dot(own_block, gate_up, preferred_element_type=jnp.float32))
    rest_hidden = activate(
        jnp.dot(blocks[0], gate_up[:half], preferred_element_type=jnp.float32)
        + jnp.dot(blocks[1], gate_up[half:], preferred_element_type=jnp.float32)
    )
    hidden = jnp.concatenate(
        [
            own_hidden.reshape(plane, 1, most, hidden_width),
            rest_hidden.reshape(plane, lines - 1, most, hidden_width),
        ],
        axis=1,
    )
    hidden = jnp.take(
        hidden, (jnp.arange(lines, dtype=jnp.int32) - here) % lines, axis=1
    ).reshape(plane * cap, hidden_width)
    mixed_parts = []
    scattered = None
    cuts = [0, width * 5 // 8, width]
    for h in range(2):
        output = jnp.dot(
            hidden, down_proj[:, cuts[h] : cuts[h + 1]], preferred_element_type=jnp.float32
        ).astype(jnp.bfloat16)
        if scattered is not None:
            scattered, output = lax.optimization_barrier((scattered, output))
        back = send(output, cap)
        back = back.reshape(plane, lines, most, cuts[h + 1] - cuts[h])
        partial = jnp.einsum(
            "bpsr,pbsd->brd", weight_hi, back, preferred_element_type=jnp.float32
        ) + jnp.einsum("bpsr,pbsd->brd", weight_lo, back, preferred_element_type=jnp.float32)
        scattered = partial.reshape(lines * rows, cuts[h + 1] - cuts[h])
        mixed_parts.append(scattered)
    for h in range(2):
        combined = lax.psum_scatter(mixed_parts[h], "tensor", scatter_dimension=0, tiled=True)
        mixed_parts[h] = x_float[:, cuts[h] : cuts[h + 1]] + combined
    mixed = jnp.concatenate(mixed_parts, axis=1).astype(jnp.bfloat16)

    local_sync = w_sync.reshape(width, -1)
    proj = jnp.dot(
        lax.all_gather(mixed, "tensor", axis=0, tiled=True),
        local_sync,
        preferred_element_type=jnp.float32,
    ).astype(jnp.bfloat16)
    half = proj.shape[1] // 2
    heads_here = head_weight.shape[0]
    head_size = half // heads_here
    frames = frame_rows.shape[2]
    clip_len = proj.shape[0]
    clip_index = jnp.arange(clip_len, dtype=jnp.int32)
    pick_audio = (frame_rows[0, 0][:, None] == clip_index[None, :]).astype(jnp.bfloat16)
    pick_video = (frame_rows[0, 1][:, None] == clip_index[None, :]).astype(jnp.bfloat16)
    audio = (
        jnp.dot(pick_audio, proj[:, :half], preferred_element_type=jnp.float32)
        .astype(jnp.bfloat16)
        .reshape(frames, heads_here, head_size)
    )
    video = (
        jnp.dot(pick_video, proj[:, half:], preferred_element_type=jnp.float32)
        .astype(jnp.bfloat16)
        .reshape(frames, heads_here, head_size)
    )
    grams = jnp.einsum("thd,shd->hts", audio, video, preferred_element_type=jnp.float32)
    times = jnp.arange(frames, dtype=jnp.int32)
    offsets = times[None, :] - times[:, None]
    diagonal = (
        (offsets[None, :, :] == lag_offsets[:, None, None])
        .astype(jnp.float32)
        .reshape(lag_offsets.shape[0], frames * frames)
    )
    sums = lax.dot_general(
        grams.reshape(heads_here, frames * frames),
        diagonal,
        (((1,), (1,)), ((), ())),
        precision=lax.Precision.HIGHEST,
        preferred_element_type=jnp.float32,
    )
    counts = (frames - jnp.abs(lag_offsets)).astype(jnp.float32)
    score = sums / jnp.sqrt(counts * head_size)[None, :]
    partial_logits = jnp.sum(head_weight[:, None] * score, axis=0)
    sync_logits = partial_logits
    step = 1
    while step < lines:
        pairs = [(i, i ^ step) for i in range(lines)]
        sync_logits = sync_logits + lax.ppermute(sync_logits, "tensor", pairs)
        step *= 2
    return (mixed, sync_logits[None, :])


def solution(mesh):
    return jax.shard_map(
        shards,
        mesh=mesh,
        in_specs=(
            P(("dp", "expert", "tensor"), None),
            P(),
            P(("dp", "expert", "tensor"), None),
            P(("dp", "expert", "tensor"), None),
            P(("dp", "expert", "tensor"), None, None),
            P(("dp", "expert", "tensor"), None, None),
            P(("dp", "expert", "tensor"), None, None),
            P(("dp", "expert", "tensor"), None, None),
            P(None, None, "tensor"),
            P("tensor"),
            P(("dp", "expert"), None, None),
            P(),
        ),
        out_specs=(P(("dp", "expert", "tensor"), None), P(("dp", "expert"), None)),
        check_vma=False,
    )
```

```python
import jax
import jax.numpy as jnp
from jax import lax
from jax.sharding import PartitionSpec as P


def dequant(weights, scales):
    block = weights.shape[0] // scales.shape[0]
    full = jnp.repeat(jnp.repeat(scales, block, axis=0), block, axis=1)
    return (weights.astype(jnp.float32) * full).astype(jnp.bfloat16)


def shards(
    tokens,
    norm_gain,
    expert_ids,
    gate_weights,
    w_in,
    scale_in,
    w_out,
    scale_out,
    w_sync,
    head_weight,
    frame_rows,
    lag_offsets,
):
    rows, width = tokens.shape
    top = expert_ids.shape[1]
    lines = lax.axis_size("tensor")
    plane = lax.axis_size(("dp", "expert"))
    experts_all = plane * lines * w_in.shape[0]
    most = 2 * rows * top // experts_all
    cap = lines * most
    here = lax.axis_index("tensor")
    x_float = tokens.astype(jnp.float32)
    normed = (
        x_float * lax.rsqrt(jnp.mean(x_float * x_float, axis=-1, keepdims=True) + 1e-06) * norm_gain
    ).astype(jnp.bfloat16)

    flat_ids = expert_ids.reshape(-1)
    pair_count = rows * top
    onehot = (flat_ids[:, None] == jnp.arange(experts_all, dtype=jnp.int32)[None, :]).astype(
        jnp.bfloat16
    )
    pair_index = jnp.arange(pair_count, dtype=jnp.int32)
    earlier = (pair_index[None, :] < pair_index[:, None]).astype(jnp.bfloat16)
    before = jnp.dot(earlier, onehot, preferred_element_type=jnp.float32)
    slots = jnp.sum(before * onehot.astype(jnp.float32), axis=1).reshape(rows, top)
    gate = gate_weights.astype(jnp.float32)
    gate_top = lax.reduce_precision(gate, exponent_bits=8, mantissa_bits=7)
    routing = jnp.concatenate(
        [
            expert_ids.astype(jnp.bfloat16),
            slots.astype(jnp.bfloat16),
            gate_top.astype(jnp.bfloat16),
            (gate - gate_top).astype(jnp.bfloat16),
        ],
        axis=1,
    )
    half = width // 2
    extra = rows * 4 * top // half
    padded = rows + 16
    packed = jnp.concatenate(
        [
            normed[:, :half],
            routing.reshape(extra, half),
            jnp.zeros((padded - rows - extra, half), jnp.bfloat16),
        ],
        axis=0,
    )
    line_a = lax.all_gather(packed, "tensor", axis=0, tiled=False)
    line_b = lax.all_gather(normed[:, half:], "tensor", axis=0, tiled=False)
    line_routing = line_a[:, rows : rows + extra, :].reshape(lines, rows, 4 * top)
    ids_l = line_routing[:, :, :top].astype(jnp.int32)
    slot_l = line_routing[:, :, top : 2 * top].astype(jnp.int32)
    gate_hi = line_routing[:, :, 2 * top : 3 * top].astype(jnp.float32)
    gate_lo = line_routing[:, :, 3 * top :].astype(jnp.float32)
    mine = (ids_l % lines) == here
    target = jnp.where(mine, (ids_l // lines) * most + slot_l, -1)
    slot_ids = jnp.arange(plane * most, dtype=jnp.int32)
    match = target[:, None, :, :] == slot_ids[None, :, None, None]
    order = (here + jnp.arange(lines, dtype=jnp.int32)) % lines
    select = jnp.any(match, axis=3).astype(jnp.bfloat16).reshape(lines, plane, most, rows)
    select_rel = jnp.take(select, order[1:], axis=0)
    weight_hi = jnp.sum(jnp.where(match, gate_hi[:, None, :, :], 0.0), axis=3)
    weight_lo = jnp.sum(jnp.where(match, gate_lo[:, None, :, :], 0.0), axis=3)
    weight_hi = weight_hi.astype(jnp.bfloat16).reshape(lines, plane, most, rows)
    weight_lo = weight_lo.astype(jnp.bfloat16).reshape(lines, plane, most, rows)
    line_parts = [
        jnp.take(line_a[:, :rows], order[1:], axis=0),
        jnp.take(line_b, order[1:], axis=0),
    ]
    own_target = jnp.where(
        (expert_ids % lines) == here,
        (expert_ids // lines) * most + slots.astype(jnp.int32),
        -1,
    )
    own_select = jnp.any(
        own_target[None, :, :] == slot_ids[:, None, None], axis=2
    ).astype(jnp.bfloat16)
    gate_up = dequant(w_in[0], scale_in[0])
    down_proj = dequant(w_out[0], scale_out[0])
    hidden_width = down_proj.shape[0]
    group = ("dp", "expert")

    def send(part, depth):
        moved = lax.all_to_all(
            part.reshape(plane, depth, part.shape[-1]), group, split_axis=0, concat_axis=0, tiled=True
        )
        return moved.reshape(plane * depth, part.shape[-1])

    own_block = send(
        jnp.dot(own_select, normed, preferred_element_type=jnp.float32).astype(jnp.bfloat16), most
    )
    blocks = [
        send(
            jnp.einsum(
                "dpsr,drD->pdsD", select_rel, line_parts[h], preferred_element_type=jnp.float32
            ).astype(jnp.bfloat16),
            cap - most,
        )
        for h in range(2)
    ]
    def activate(mixed_in):
        return (jax.nn.silu(mixed_in[:, :hidden_width]) * mixed_in[:, hidden_width:]).astype(
            jnp.bfloat16
        )

    own_hidden = activate(jnp.dot(own_block, gate_up, preferred_element_type=jnp.float32))
    rest_hidden = activate(
        jnp.dot(blocks[0], gate_up[:half], preferred_element_type=jnp.float32)
        + jnp.dot(blocks[1], gate_up[half:], preferred_element_type=jnp.float32)
    )
    hidden = jnp.concatenate(
        [
            own_hidden.reshape(plane, 1, most, hidden_width),
            rest_hidden.reshape(plane, lines - 1, most, hidden_width),
        ],
        axis=1,
    )
    hidden = jnp.take(
        hidden, (jnp.arange(lines, dtype=jnp.int32) - here) % lines, axis=1
    ).reshape(plane * cap, hidden_width)
    mixed_parts = []
    scattered = None
    cuts = [0, width * 9 // 16, width]
    for h in range(2):
        output = jnp.dot(
            hidden, down_proj[:, cuts[h] : cuts[h + 1]], preferred_element_type=jnp.float32
        ).astype(jnp.bfloat16)
        if scattered is not None:
            scattered, output = lax.optimization_barrier((scattered, output))
        back = send(output, cap)
        back = back.reshape(plane, lines, most, cuts[h + 1] - cuts[h])
        partial = jnp.einsum(
            "bpsr,pbsd->brd", weight_hi, back, preferred_element_type=jnp.float32
        ) + jnp.einsum("bpsr,pbsd->brd", weight_lo, back, preferred_element_type=jnp.float32)
        scattered = partial.reshape(lines * rows, cuts[h + 1] - cuts[h])
        mixed_parts.append(scattered)
    for h in range(2):
        combined = lax.psum_scatter(mixed_parts[h], "tensor", scatter_dimension=0, tiled=True)
        mixed_parts[h] = x_float[:, cuts[h] : cuts[h + 1]] + combined
    mixed = jnp.concatenate(mixed_parts, axis=1).astype(jnp.bfloat16)

    local_sync = w_sync.reshape(width, -1)
    proj = jnp.dot(
        lax.all_gather(mixed, "tensor", axis=0, tiled=True),
        local_sync,
        preferred_element_type=jnp.float32,
    ).astype(jnp.bfloat16)
    half = proj.shape[1] // 2
    heads_here = head_weight.shape[0]
    head_size = half // heads_here
    frames = frame_rows.shape[2]
    clip_len = proj.shape[0]
    clip_index = jnp.arange(clip_len, dtype=jnp.int32)
    pick_audio = (frame_rows[0, 0][:, None] == clip_index[None, :]).astype(jnp.bfloat16)
    pick_video = (frame_rows[0, 1][:, None] == clip_index[None, :]).astype(jnp.bfloat16)
    audio = (
        jnp.dot(pick_audio, proj[:, :half], preferred_element_type=jnp.float32)
        .astype(jnp.bfloat16)
        .reshape(frames, heads_here, head_size)
    )
    video = (
        jnp.dot(pick_video, proj[:, half:], preferred_element_type=jnp.float32)
        .astype(jnp.bfloat16)
        .reshape(frames, heads_here, head_size)
    )
    grams = jnp.einsum("thd,shd->hts", audio, video, preferred_element_type=jnp.float32)
    times = jnp.arange(frames, dtype=jnp.int32)
    offsets = times[None, :] - times[:, None]
    diagonal = (
        (offsets[None, :, :] == lag_offsets[:, None, None])
        .astype(jnp.float32)
        .reshape(lag_offsets.shape[0], frames * frames)
    )
    sums = lax.dot_general(
        grams.reshape(heads_here, frames * frames),
        diagonal,
        (((1,), (1,)), ((), ())),
        precision=lax.Precision.HIGHEST,
        preferred_element_type=jnp.float32,
    )
    counts = (frames - jnp.abs(lag_offsets)).astype(jnp.float32)
    score = sums / jnp.sqrt(counts * head_size)[None, :]
    partial_logits = jnp.sum(head_weight[:, None] * score, axis=0)
    sync_logits = partial_logits
    step = 1
    while step < lines:
        pairs = [(i, i ^ step) for i in range(lines)]
        sync_logits = sync_logits + lax.ppermute(sync_logits, "tensor", pairs)
        step *= 2
    return (mixed, sync_logits[None, :])


def solution(mesh):
    return jax.shard_map(
        shards,
        mesh=mesh,
        in_specs=(
            P(("dp", "expert", "tensor"), None),
            P(),
            P(("dp", "expert", "tensor"), None),
            P(("dp", "expert", "tensor"), None),
            P(("dp", "expert", "tensor"), None, None),
            P(("dp", "expert", "tensor"), None, None),
            P(("dp", "expert", "tensor"), None, None),
            P(("dp", "expert", "tensor"), None, None),
            P(None, None, "tensor"),
            P("tensor"),
            P(("dp", "expert"), None, None),
            P(),
        ),
        out_specs=(P(("dp", "expert", "tensor"), None), P(("dp", "expert"), None)),
        check_vma=False,
    )
```

```python
import jax
import jax.numpy as jnp
from jax import lax
from jax.sharding import PartitionSpec as P


def dequant(weights, scales):
    block = weights.shape[0] // scales.shape[0]
    full = jnp.repeat(jnp.repeat(scales, block, axis=0), block, axis=1)
    return (weights.astype(jnp.float32) * full).astype(jnp.bfloat16)


def shards(
    tokens,
    norm_gain,
    expert_ids,
    gate_weights,
    w_in,
    scale_in,
    w_out,
    scale_out,
    w_sync,
    head_weight,
    frame_rows,
    lag_offsets,
):
    rows, width = tokens.shape
    top = expert_ids.shape[1]
    lines = lax.axis_size("tensor")
    plane = lax.axis_size(("dp", "expert"))
    experts_all = plane * lines * w_in.shape[0]
    most = 2 * rows * top // experts_all
    cap = lines * most
    here = lax.axis_index("tensor")
    x_float = tokens.astype(jnp.float32)
    normed = (
        x_float * lax.rsqrt(jnp.mean(x_float * x_float, axis=-1, keepdims=True) + 1e-06) * norm_gain
    ).astype(jnp.bfloat16)

    flat_ids = expert_ids.reshape(-1)
    pair_count = rows * top
    onehot = (flat_ids[:, None] == jnp.arange(experts_all, dtype=jnp.int32)[None, :]).astype(
        jnp.bfloat16
    )
    pair_index = jnp.arange(pair_count, dtype=jnp.int32)
    earlier = (pair_index[None, :] < pair_index[:, None]).astype(jnp.bfloat16)
    before = jnp.dot(earlier, onehot, preferred_element_type=jnp.float32)
    slots = jnp.sum(before * onehot.astype(jnp.float32), axis=1).reshape(rows, top)
    gate = gate_weights.astype(jnp.float32)
    gate_top = lax.reduce_precision(gate, exponent_bits=8, mantissa_bits=7)
    routing = jnp.concatenate(
        [
            expert_ids.astype(jnp.bfloat16),
            slots.astype(jnp.bfloat16),
            gate_top.astype(jnp.bfloat16),
            (gate - gate_top).astype(jnp.bfloat16),
        ],
        axis=1,
    )
    half = width // 2
    extra = rows * 4 * top // half
    padded = rows + 16
    packed = jnp.concatenate(
        [
            normed[:, :half],
            routing.reshape(extra, half),
            jnp.zeros((padded - rows - extra, half), jnp.bfloat16),
        ],
        axis=0,
    )
    line_a = lax.all_gather(packed, "tensor", axis=0, tiled=False)
    line_b = lax.all_gather(normed[:, half:], "tensor", axis=0, tiled=False)
    line_routing = line_a[:, rows : rows + extra, :].reshape(lines, rows, 4 * top)
    ids_l = line_routing[:, :, :top].astype(jnp.int32)
    slot_l = line_routing[:, :, top : 2 * top].astype(jnp.int32)
    gate_hi = line_routing[:, :, 2 * top : 3 * top].astype(jnp.float32)
    gate_lo = line_routing[:, :, 3 * top :].astype(jnp.float32)
    mine = (ids_l % lines) == here
    target = jnp.where(mine, (ids_l // lines) * most + slot_l, -1)
    slot_ids = jnp.arange(plane * most, dtype=jnp.int32)
    match = target[:, None, :, :] == slot_ids[None, :, None, None]
    order = (here + jnp.arange(lines, dtype=jnp.int32)) % lines
    select = jnp.any(match, axis=3).astype(jnp.bfloat16).reshape(lines, plane, most, rows)
    select_rel = jnp.take(select, order[1:], axis=0)
    weight_hi = jnp.sum(jnp.where(match, gate_hi[:, None, :, :], 0.0), axis=3)
    weight_lo = jnp.sum(jnp.where(match, gate_lo[:, None, :, :], 0.0), axis=3)
    weight_hi = weight_hi.astype(jnp.bfloat16).reshape(lines, plane, most, rows)
    weight_lo = weight_lo.astype(jnp.bfloat16).reshape(lines, plane, most, rows)
    line_parts = [
        jnp.take(line_a[:, :rows], order[1:], axis=0),
        jnp.take(line_b, order[1:], axis=0),
    ]
    own_target = jnp.where(
        (expert_ids % lines) == here,
        (expert_ids // lines) * most + slots.astype(jnp.int32),
        -1,
    )
    own_select = jnp.any(
        own_target[None, :, :] == slot_ids[:, None, None], axis=2
    ).astype(jnp.bfloat16)
    gate_up = dequant(w_in[0], scale_in[0])
    down_proj = dequant(w_out[0], scale_out[0])
    hidden_width = down_proj.shape[0]
    group = ("dp", "expert")

    def send(part, depth):
        moved = lax.all_to_all(
            part.reshape(plane, depth, part.shape[-1]), group, split_axis=0, concat_axis=0, tiled=True
        )
        return moved.reshape(plane * depth, part.shape[-1])

    own_block = send(
        jnp.dot(own_select, normed, preferred_element_type=jnp.float32).astype(jnp.bfloat16), most
    )
    blocks = [
        send(
            jnp.einsum(
                "dpsr,drD->pdsD", select_rel, line_parts[h], preferred_element_type=jnp.float32
            ).astype(jnp.bfloat16),
            cap - most,
        )
        for h in range(2)
    ]
    def activate(mixed_in):
        return (jax.nn.silu(mixed_in[:, :hidden_width]) * mixed_in[:, hidden_width:]).astype(
            jnp.bfloat16
        )

    own_hidden = activate(jnp.dot(own_block, gate_up, preferred_element_type=jnp.float32))
    rest_hidden = activate(
        jnp.dot(blocks[0], gate_up[:half], preferred_element_type=jnp.float32)
        + jnp.dot(blocks[1], gate_up[half:], preferred_element_type=jnp.float32)
    )
    hidden = jnp.concatenate(
        [
            own_hidden.reshape(plane, 1, most, hidden_width),
            rest_hidden.reshape(plane, lines - 1, most, hidden_width),
        ],
        axis=1,
    )
    hidden = jnp.take(
        hidden, (jnp.arange(lines, dtype=jnp.int32) - here) % lines, axis=1
    ).reshape(plane * cap, hidden_width)
    mixed_parts = []
    scattered = None
    cuts = [0, width * 9 // 16, width]
    for h in range(2):
        output = jnp.dot(
            hidden, down_proj[:, cuts[h] : cuts[h + 1]], preferred_element_type=jnp.float32
        ).astype(jnp.bfloat16)
        if scattered is not None:
            scattered, output = lax.optimization_barrier((scattered, output))
        back = send(output, cap)
        back = back.reshape(plane, lines, most, cuts[h + 1] - cuts[h])
        partial = jnp.einsum(
            "bpsr,pbsd->brd", weight_hi, back, preferred_element_type=jnp.float32
        ) + jnp.einsum("bpsr,pbsd->brd", weight_lo, back, preferred_element_type=jnp.float32)
        scattered = partial.reshape(lines * rows, cuts[h + 1] - cuts[h])
        mixed_parts.append(scattered)
    for h in range(2):
        combined = lax.psum_scatter(mixed_parts[h], "tensor", scatter_dimension=0, tiled=True)
        mixed_parts[h] = x_float[:, cuts[h] : cuts[h + 1]] + combined
    mixed = jnp.concatenate(mixed_parts, axis=1).astype(jnp.bfloat16)

    local_sync = w_sync.reshape(width, -1)
    proj = jnp.dot(
        lax.all_gather(mixed, "tensor", axis=0, tiled=True),
        local_sync,
        preferred_element_type=jnp.float32,
    ).astype(jnp.bfloat16)
    half = proj.shape[1] // 2
    heads_here = head_weight.shape[0]
    head_size = half // heads_here
    frames = frame_rows.shape[2]
    clip_len = proj.shape[0]
    clip_index = jnp.arange(clip_len, dtype=jnp.int32)
    pick_audio = (frame_rows[0, 0][:, None] == clip_index[None, :]).astype(jnp.bfloat16)
    pick_video = (frame_rows[0, 1][:, None] == clip_index[None, :]).astype(jnp.bfloat16)
    audio = (
        jnp.dot(pick_audio, proj[:, :half], preferred_element_type=jnp.float32)
        .astype(jnp.bfloat16)
        .reshape(frames, heads_here, head_size)
    )
    video = (
        jnp.dot(pick_video, proj[:, half:], preferred_element_type=jnp.float32)
        .astype(jnp.bfloat16)
        .reshape(frames, heads_here, head_size)
    )
    grams = jnp.einsum("thd,shd->hts", audio, video, preferred_element_type=jnp.float32)
    times = jnp.arange(frames, dtype=jnp.int32)
    offsets = times[None, :] - times[:, None]
    diagonal = (
        (offsets[None, :, :] == lag_offsets[:, None, None])
        .astype(jnp.float32)
        .reshape(lag_offsets.shape[0], frames * frames)
    )
    sums = lax.dot_general(
        grams.reshape(heads_here, frames * frames),
        diagonal,
        (((1,), (1,)), ((), ())),
        precision=lax.Precision.HIGHEST,
        preferred_element_type=jnp.float32,
    )
    counts = (frames - jnp.abs(lag_offsets)).astype(jnp.float32)
    score = sums / jnp.sqrt(counts * head_size)[None, :]
    partial_logits = jnp.sum(head_weight[:, None] * score, axis=0)
    received = [partial_logits] + [
        lax.ppermute(partial_logits, "tensor", [(i, (i + k) % lines) for i in range(lines)])
        for k in range(1, lines)
    ]
    stacked = jnp.stack(received)
    ordered = jnp.take(stacked, (here - jnp.arange(lines, dtype=jnp.int32)) % lines, axis=0)
    sync_logits = ordered[0]
    for j in range(1, lines):
        sync_logits = sync_logits + ordered[j]
    return (mixed, sync_logits[None, :])


def solution(mesh):
    return jax.shard_map(
        shards,
        mesh=mesh,
        in_specs=(
            P(("dp", "expert", "tensor"), None),
            P(),
            P(("dp", "expert", "tensor"), None),
            P(("dp", "expert", "tensor"), None),
            P(("dp", "expert", "tensor"), None, None),
            P(("dp", "expert", "tensor"), None, None),
            P(("dp", "expert", "tensor"), None, None),
            P(("dp", "expert", "tensor"), None, None),
            P(None, None, "tensor"),
            P("tensor"),
            P(("dp", "expert"), None, None),
            P(),
        ),
        out_specs=(P(("dp", "expert", "tensor"), None), P(("dp", "expert"), None)),
        check_vma=False,
    )
```
